32 devices in a mesh: req: 4 (over x, core), head: 8 (over z, y).
Axes of the slice: x: 2, y: 2, z: 4, core: 2. Of those that a mesh axis runs over, the one named last changes fastest.
Arguments:
- stretch_acts: bfloat16 [8, 256, 2048], P(None, ('req', 'head')), may hold values from -6 to 6
- cache_prefill: bfloat16 [8, 8, 256, 32, 128], P('req', None, 'head'), may hold values from -600 to 600
- stretch_lens: int32 [8], replicated, may hold values from 1 to 256, 1280 in all
- prefix_lens: int32 [8], replicated, may hold values from 1 to 256, 1280 in all
- req_order: int32 [8], replicated, may hold values from 0 to 7, each once
- attn_gain: bfloat16 [2048], replicated, may hold values from 0.25 to 1.75
- in_weight: bfloat16 [2048, 32, 192], P(None, 'head'), may hold values from -0.125 to 0.125
- slopes: float32 [32], P('head'), may hold values from 0.00390625 to 0.5
- out_weight: bfloat16 [32, 64, 2048], P('head'), may hold values from -0.125 to 0.125
- mlp_gain: bfloat16 [2048], replicated, may hold values from 0.25 to 1.75
- up_weight: bfloat16 [2048, 8192], P(None, 'head'), may hold values from -0.125 to 0.125
- down_weight: bfloat16 [8192, 2048], P('head'), may hold values from -0.0625 to 0.0625
Outputs:
- layer_out: bfloat16 [8, 256, 2048], P(None, ('req', 'head'))
- cache_decode: bfloat16 [8, 8, 256, 32, 128], P(None, 'req', None, 'head')
The draws below stay inside these ranges and needn't reach their ends.
Inputs may be any that keep to these rules, and one draw needn't show every extreme that they name: `stretch_lens`: the entries sum to 1280 and the largest is exactly 256. `prefix_lens`: the entries sum to 1280 and the largest is exactly 256. `req_order`: each request appears once.
All inputs are finite; a program needn't handle non-finite values.
Results may differ from the reference program's by a relative error of at most 0.013.
The reference program's roundings to bfloat16 on the way (of `normed`, `mixed`, `soft`, `context`, `normed_mlp` and `inner`) count: a program that leaves them out, or rounds other values in their place, can miss the bound.
Values may be sent and summed in bfloat16 or wider, within the bound.
No kernel may reach another device: no remote copies, remote signals or barrier semaphores. Data moves between devices by JAX's collectives and lax.ppermute only.
A program may use at most 128 MiB of HBM per device.

```python
import math
import jax
import jax.numpy as jnp
import numpy as np
from jax import lax

D = 2048
HEADS = 32
HD = 64
FF = 8192
REQS = 8
LAYERS = 8
CMAX = 256
PMAX = 256
N_HEAD = 8


def draw_cache_prefill(key, part):
    first_key = jax.random.fold_in(jax.random.fold_in(key, 7), 0)
    shape = (LAYERS, REQS, PMAX, HEADS, 2 * HD)
    base = jnp.clip(jax.random.normal(first_key, shape, jnp.float32), -6.0, 6.0)
    return base.astype(jnp.bfloat16)


def level_of(rng, extent, cuts, least, top_value):
    level, own = 1.0, jax.random.fold_in(rng, 6)
    for position, parts in cuts:
        draws = jnp.exp(jax.random.uniform(jax.random.fold_in(own, position), (parts,), jnp.float32, least / len(cuts), top_value / len(cuts)))
        level = level * jnp.repeat(draws, extent[position] // parts).reshape([-1 if axis == position else 1 for axis in range(len(extent))])
    return level


def profile(count, total, bound, lean):
    portions = [(1 << 20) // math.isqrt(rank ** lean) + 1 for rank in range(2, count + 1)]
    spare, holding = total - bound - (count - 1), [1] * (count - 1)
    while spare > 0:
        candidates = [i for i in range(count - 1) if holding[i] < bound]
        whole, remaining = sum([portions[i] for i in candidates]), spare
        for i in candidates:
            addition = min(bound - holding[i], max(1, remaining * portions[i] // whole), spare)
            holding[i] = holding[i] + addition
            spare = spare - addition
    return np.array([bound] + holding)


def ragged(own_key, count, total, most, lean):
    if count == 2:
        one = jax.random.randint(own_key, (), max(1, total - most), min(most, total - 1) + 1)
        return jnp.stack([one, total - one])
    sizes = jnp.asarray(profile(count, total, most, lean), jnp.int32)
    twos = (count - 1) // 2
    source_of, sink = sizes[1:1 + 2 * twos:2], sizes[2:2 + 2 * twos:2]
    slack = jnp.minimum(source_of - 1, most - sink)
    shifted = jax.random.randint(jax.random.fold_in(own_key, 1), (twos,), 0, 1 << 20) % (slack + 1)
    sizes = sizes.at[1:1 + 2 * twos:2].set(source_of - shifted).at[2:2 + 2 * twos:2].set(sink + shifted)
    return sizes[jax.random.permutation(jax.random.fold_in(own_key, 2), count)]


def noise(own_key, shape, scale, most, shards=(), kind=jnp.bfloat16):
    array = scale * jax.random.normal(own_key, shape, jnp.float32)
    if shards:
        array = array * level_of(own_key, shape, shards, -0.22, 0.18)
    return jnp.clip(array, -most, most).astype(kind)


def setup_inputs(seed: int = 0) -> dict:
    keys = jax.random.split(jax.random.key(seed), 13)
    stretch_acts = noise(keys[0], (REQS, CMAX, D), 1.0, 6.0, ((1, 32),))
    cache_prefill = draw_cache_prefill(jax.random.fold_in(keys[12], 71), 0)
    stretch_lens = ragged(keys[2], REQS, 5 * REQS * CMAX // 8, CMAX, 2).astype(jnp.int32)
    prefix_lens = ragged(keys[3], REQS, 5 * REQS * PMAX // 8, PMAX, 2).astype(jnp.int32)
    req_order = jax.random.permutation(keys[4], REQS).astype(jnp.int32)
    attn_gain = jnp.clip(1.0 + 0.15 * jax.random.normal(keys[5], (D,), jnp.float32), 0.25, 1.75).astype(jnp.bfloat16)
    in_weight = noise(keys[6], (D, HEADS, 3 * HD), D ** -0.5, 0.125, ((1, 8),))
    slopes = jnp.clip(jnp.exp(math.log(0.5) - 4.8520303 * jax.random.uniform(keys[7], (HEADS,), jnp.float32) ** level_of(keys[7], (HEADS,), ((0, 8),), -0.2, 0.2)), 0.00390625, 0.5)
    out_weight = noise(keys[8], (HEADS, HD, D), (HEADS * HD) ** -0.5, 0.125, ((0, 8),))
    mlp_gain = jnp.clip(1.0 + 0.15 * jax.random.normal(keys[9], (D,), jnp.float32), 0.25, 1.75).astype(jnp.bfloat16)
    up_weight = noise(keys[10], (D, FF), D ** -0.5, 0.125, ((1, 8),))
    down_weight = noise(keys[11], (FF, D), FF ** -0.5, 0.0625, ((0, 8),))
    return {"stretch_acts": stretch_acts, "cache_prefill": cache_prefill, "stretch_lens": stretch_lens, "prefix_lens": prefix_lens, "req_order": req_order, "attn_gain": attn_gain, "in_weight": in_weight, "slopes": slopes, "out_weight": out_weight, "mlp_gain": mlp_gain, "up_weight": up_weight, "down_weight": down_weight}


EPSILON = 1e-05

def layer_norm(values, gain):
    average = lax.optimization_barrier(jnp.mean(values, axis=-1, keepdims=True))
    centred = values - average
    variance = lax.optimization_barrier(jnp.mean(centred * centred, axis=-1, keepdims=True))
    return centred * lax.rsqrt(variance + EPSILON) * gain.astype(jnp.float32)

def rounded(values):
    return lax.optimization_barrier(values.astype(jnp.bfloat16)).astype(jnp.float32)

def group_sum(acts, weight, groups):
    span = acts.shape[1] // groups
    acts_split = acts.reshape(acts.shape[0], groups, span).transpose(1, 0, 2)
    weight_split = weight.reshape(groups, span, weight.shape[1])

    def add_group(summed, pair):
        piece = jnp.dot(pair[0], pair[1], preferred_element_type=jnp.float32)
        return (summed + rounded(piece), None)
    start = jnp.zeros((acts.shape[0], weight.shape[1]), jnp.float32)
    summed, unused = lax.scan(add_group, start, (acts_split, weight_split))
    return summed

def attend(queries, pairs, prefix_len, slopes, head_dim):
    stretch = queries.shape[0]
    prefix = pairs.shape[0] - stretch
    keys_part = pairs[..., :head_dim]
    values_part = pairs[..., head_dim:]
    scores = jnp.einsum('qhd,khd->hqk', queries.astype(jnp.float32), keys_part.astype(jnp.float32)) * (1.0 / math.sqrt(head_dim))
    row_index = jnp.arange(stretch, dtype=jnp.int32)
    key_index = jnp.arange(prefix + stretch, dtype=jnp.int32)
    in_prefix = key_index < prefix
    query_pos = prefix_len + row_index
    key_pos = jnp.where(in_prefix, key_index, prefix_len + key_index - prefix)
    allowed = jnp.where(in_prefix[None, :], key_index[None, :] < prefix_len, (key_index - prefix)[None, :] <= row_index[:, None])
    distance = (query_pos[:, None] - key_pos[None, :]).astype(jnp.float32)
    scores = scores - slopes.astype(jnp.float32)[:, None, None] * distance[None]
    scores = jnp.where(allowed[None], scores, -jnp.inf)
    highest = lax.optimization_barrier(jnp.max(scores, axis=-1, keepdims=True))
    expo = jnp.exp(scores - highest)
    soft = (expo / lax.optimization_barrier(jnp.sum(expo, axis=-1, keepdims=True))).astype(jnp.bfloat16)
    context = jnp.einsum('hqk,khd->qhd', soft.astype(jnp.float32), values_part.astype(jnp.float32))
    return context.astype(jnp.bfloat16).reshape(stretch, -1)

def reference(stretch_acts, cache_prefill, stretch_lens, prefix_lens, req_order, attn_gain, in_weight, slopes, out_weight, mlp_gain, up_weight, down_weight):
    positions = jnp.arange(PMAX, dtype=jnp.int32)
    keep = positions[None, :] < prefix_lens[:, None]
    masked = jnp.where(keep[None, :, :, None, None], cache_prefill, jnp.zeros((), cache_prefill.dtype))
    cache_decode = jnp.take(masked, req_order, axis=1)
    rows = jnp.arange(CMAX, dtype=jnp.int32)
    outputs = []
    for request in range(REQS):
        acts = stretch_acts[request].astype(jnp.float32)
        normed = layer_norm(acts, attn_gain).astype(jnp.bfloat16)
        mixed = jnp.dot(normed, in_weight.reshape(D, HEADS * 3 * HD), preferred_element_type=jnp.float32)
        mixed = mixed.reshape(CMAX, HEADS, 3 * HD).astype(jnp.bfloat16)
        pairs = jnp.concatenate([masked[0, request], mixed[:, :, HD:]], axis=0)
        context = attend(mixed[:, :, :HD], pairs, prefix_lens[request], slopes, HD)
        attn = group_sum(context, out_weight.reshape(HEADS * HD, D), N_HEAD)
        residual = acts + attn
        normed_mlp = layer_norm(residual, mlp_gain).astype(jnp.bfloat16)
        inner = jax.nn.gelu(jnp.dot(normed_mlp, up_weight, preferred_element_type=jnp.float32), approximate=False).astype(jnp.bfloat16)
        mlp = group_sum(inner, down_weight, N_HEAD)
        usable = rows < stretch_lens[request]
        outputs.append(jnp.where(usable[:, None], residual + mlp, jnp.zeros((), jnp.float32)).astype(jnp.bfloat16))
    return (jnp.stack(outputs), cache_decode)
```

```python
import math

import jax
import jax.numpy as jnp
from jax import lax
from jax.sharding import PartitionSpec as P

EPSILON = 1e-05


def layer_norm(values, gain):
    average = jnp.mean(values, axis=-1, keepdims=True)
    centred = values - average
    variance = jnp.mean(centred * centred, axis=-1, keepdims=True)
    return centred * lax.rsqrt(variance + EPSILON) * gain.astype(jnp.float32)


def attend(queries, pairs, prefix_len, slopes, head_dim):
    stretch = queries.shape[0]
    prefix = pairs.shape[0] - stretch
    keys_part = pairs[..., :head_dim]
    values_part = pairs[..., head_dim:]
    scores = jnp.einsum("qhd,khd->hqk", queries, keys_part, preferred_element_type=jnp.float32) * (
        1.0 / math.sqrt(head_dim)
    )
    row_index = jnp.arange(stretch, dtype=jnp.int32)
    key_index = jnp.arange(prefix + stretch, dtype=jnp.int32)
    in_prefix = key_index < prefix
    query_pos = prefix_len + row_index
    key_pos = jnp.where(in_prefix, key_index, prefix_len + key_index - prefix)
    allowed = jnp.where(
        in_prefix[None, :],
        key_index[None, :] < prefix_len,
        (key_index - prefix)[None, :] <= row_index[:, None],
    )
    distance = (query_pos[:, None] - key_pos[None, :]).astype(jnp.float32)
    scores = scores - slopes[:, None, None] * distance[None]
    scores = jnp.where(allowed[None], scores, -jnp.inf)
    highest = jnp.max(scores, axis=-1, keepdims=True)
    expo = jnp.exp(scores - highest)
    soft = (expo / jnp.sum(expo, axis=-1, keepdims=True)).astype(jnp.bfloat16)
    context = jnp.einsum("hqk,khd->qhd", soft, values_part, preferred_element_type=jnp.float32)
    return context.astype(jnp.bfloat16).reshape(stretch, -1)


def local(
    stretch_acts,
    cache_prefill,
    stretch_lens,
    prefix_lens,
    req_order,
    attn_gain,
    in_weight,
    slopes,
    out_weight,
    mlp_gain,
    up_weight,
    down_weight,
):
    req_count = lax.axis_size("req")
    head_count = lax.axis_size("head")
    req_index = lax.axis_index("req")
    head_index = lax.axis_index("head")
    requests = stretch_acts.shape[0]
    stretch_rows = stretch_acts.shape[1]
    features = stretch_acts.shape[2]
    group_size = requests // req_count
    span_rows = head_count * stretch_rows
    stretch_max = req_count * span_rows
    prefix_rows = cache_prefill.shape[2]
    heads_here = in_weight.shape[1]
    pair_width = cache_prefill.shape[4]
    head_dim = pair_width // 2
    members = lax.dynamic_slice_in_dim(req_order, req_index * group_size, group_size)
    member_stretch = jnp.take(stretch_lens, members)
    member_prefix = jnp.take(prefix_lens, members)
    ordered_prefix = jnp.take(prefix_lens, req_order)
    positions = head_index * prefix_rows + jnp.arange(prefix_rows, dtype=jnp.int32)
    keep = positions[None, :] < ordered_prefix[:, None]
    local_layers = cache_prefill.shape[0]
    halves = []
    for layer in range(local_layers):
        dealt_cache = jnp.where(
            keep[None, :, :, None, None],
            jnp.take(cache_prefill[layer : layer + 1], req_order, axis=1),
            jnp.zeros((), cache_prefill.dtype),
        )
        halves.append(
            lax.all_to_all(
                lax.all_to_all(dealt_cache, "head", split_axis=3, concat_axis=2, tiled=True),
                "req",
                split_axis=1,
                concat_axis=0,
                tiled=True,
            )
        )
    current = halves[0][0]
    relaid = jnp.stack(halves, axis=1).reshape((req_count * local_layers,) + halves[0].shape[1:])
    dealt_acts = jnp.take(stretch_acts, req_order, axis=0)
    dealt_rows = lax.all_to_all(dealt_acts, "req", split_axis=0, concat_axis=1, tiled=True).reshape(
        group_size, req_count, stretch_rows, features
    )
    gathered = lax.all_gather(dealt_rows, "head", axis=2, tiled=True)
    normed = (
        layer_norm(gathered.astype(jnp.float32), attn_gain)
        .astype(jnp.bfloat16)
        .reshape(group_size * stretch_max, features)
    )
    mixed = jnp.dot(
        normed,
        in_weight.reshape(features, heads_here * 3 * head_dim),
        preferred_element_type=jnp.float32,
    )
    mixed = mixed.reshape(group_size, stretch_max, heads_here, 3 * head_dim).astype(jnp.bfloat16)
    contexts = []
    for member in range(group_size):
        pairs = jnp.concatenate([current[member], mixed[member, :, :, head_dim:]], axis=0)
        contexts.append(
            attend(mixed[member, :, :, :head_dim], pairs, member_prefix[member], slopes, head_dim)
        )
    context = jnp.concatenate(contexts, axis=0)
    partial_attn = jnp.dot(
        context,
        out_weight.reshape(heads_here * head_dim, features),
        preferred_element_type=jnp.float32,
    )
    partial_attn = partial_attn.reshape(group_size, req_count, span_rows, features)
    attn_rows = lax.psum_scatter(
        partial_attn.astype(jnp.bfloat16), "head", scatter_dimension=2, tiled=True
    ).astype(jnp.float32)
    residual_rows = dealt_rows.astype(jnp.float32) + attn_rows
    normed_rows = layer_norm(residual_rows, mlp_gain).astype(jnp.bfloat16)
    normed_all = lax.all_gather(normed_rows, "head", axis=2, tiled=True)
    inner = jax.nn.gelu(
        jnp.dot(
            normed_all.reshape(group_size * stretch_max, features),
            up_weight,
            preferred_element_type=jnp.float32,
        ),
        approximate=False,
    ).astype(jnp.bfloat16)
    partial_mlp = jnp.dot(inner, down_weight, preferred_element_type=jnp.float32).reshape(
        group_size, req_count, span_rows, features
    )
    mlp_rows = lax.psum_scatter(
        partial_mlp.astype(jnp.bfloat16), "head", scatter_dimension=2, tiled=True
    ).astype(jnp.float32)
    row_number = (
        jnp.arange(req_count, dtype=jnp.int32)[:, None] * head_count + head_index
    ) * stretch_rows + jnp.arange(stretch_rows, dtype=jnp.int32)[None, :]
    usable = row_number[None] < member_stretch[:, None, None]
    result = jnp.where(
        usable[..., None], residual_rows + mlp_rows, jnp.zeros((), jnp.float32)
    ).astype(jnp.bfloat16)
    returned = lax.all_to_all(result, "req", split_axis=1, concat_axis=0, tiled=True).reshape(
        requests, stretch_rows, features
    )
    inverse = jnp.argsort(req_order)
    layer_out = jnp.take(returned, inverse, axis=0)
    return (layer_out, relaid)


def solution(mesh):
    return jax.shard_map(
        local,
        mesh=mesh,
        in_specs=(
            P(None, ("req", "head"), None),
            P("req", None, "head", None, None),
            P(),
            P(),
            P(),
            P(),
            P(None, "head", None),
            P("head"),
            P("head", None, None),
            P(),
            P(None, "head"),
            P("head", None),
        ),
        out_specs=(P(None, ("req", "head"), None), P(None, "req", None, "head", None)),
        check_vma=False,
    )
```

```python
import math

import jax
import jax.numpy as jnp
from jax import lax
from jax.sharding import PartitionSpec as P

EPSILON = 1e-05


def layer_norm(values, gain):
    average = jnp.mean(values, axis=-1, keepdims=True)
    centred = values - average
    variance = jnp.mean(centred * centred, axis=-1, keepdims=True)
    return centred * lax.rsqrt(variance + EPSILON) * gain.astype(jnp.float32)


def attend(queries, pairs, prefix_len, slopes, head_dim):
    stretch = queries.shape[0]
    prefix = pairs.shape[0] - stretch
    keys_part = pairs[..., :head_dim]
    values_part = pairs[..., head_dim:]
    scores = jnp.einsum("qhd,khd->hqk", queries, keys_part, preferred_element_type=jnp.float32) * (
        1.0 / math.sqrt(head_dim)
    )
    row_index = jnp.arange(stretch, dtype=jnp.int32)
    key_index = jnp.arange(prefix + stretch, dtype=jnp.int32)
    in_prefix = key_index < prefix
    query_pos = prefix_len + row_index
    key_pos = jnp.where(in_prefix, key_index, prefix_len + key_index - prefix)
    allowed = jnp.where(
        in_prefix[None, :],
        key_index[None, :] < prefix_len,
        (key_index - prefix)[None, :] <= row_index[:, None],
    )
    distance = (query_pos[:, None] - key_pos[None, :]).astype(jnp.float32)
    scores = scores - slopes[:, None, None] * distance[None]
    scores = jnp.where(allowed[None], scores, -jnp.inf)
    highest = jnp.max(scores, axis=-1, keepdims=True)
    expo = jnp.exp(scores - highest)
    soft = (expo / jnp.sum(expo, axis=-1, keepdims=True)).astype(jnp.bfloat16)
    context = jnp.einsum("hqk,khd->qhd", soft, values_part, preferred_element_type=jnp.float32)
    return context.astype(jnp.bfloat16).reshape(stretch, -1)


def local(
    stretch_acts,
    cache_prefill,
    stretch_lens,
    prefix_lens,
    req_order,
    attn_gain,
    in_weight,
    slopes,
    out_weight,
    mlp_gain,
    up_weight,
    down_weight,
):
    req_count = lax.axis_size("req")
    head_count = lax.axis_size("head")
    req_index = lax.axis_index("req")
    head_index = lax.axis_index("head")
    requests = stretch_acts.shape[0]
    stretch_rows = stretch_acts.shape[1]
    features = stretch_acts.shape[2]
    group_size = requests // req_count
    span_rows = head_count * stretch_rows
    stretch_max = req_count * span_rows
    prefix_rows = cache_prefill.shape[2]
    heads_here = in_weight.shape[1]
    pair_width = cache_prefill.shape[4]
    head_dim = pair_width // 2
    members = lax.dynamic_slice_in_dim(req_order, req_index * group_size, group_size)
    member_stretch = jnp.take(stretch_lens, members)
    member_prefix = jnp.take(prefix_lens, members)
    ordered_prefix = jnp.take(prefix_lens, req_order)
    positions = head_index * prefix_rows + jnp.arange(prefix_rows, dtype=jnp.int32)
    keep = positions[None, :] < ordered_prefix[:, None]
    local_layers = cache_prefill.shape[0]
    slots = cache_prefill.shape[1]
    heads = cache_prefill.shape[3]
    devices = req_count * head_count
    chunks = []
    for layer in range(local_layers):
        dealt_cache = jnp.where(
            keep[:, :, None, None],
            jnp.take(cache_prefill[layer], req_order, axis=0),
            jnp.zeros((), cache_prefill.dtype),
        )
        outgoing = (
            dealt_cache.reshape(req_count, group_size, prefix_rows, head_count, heads // head_count, pair_width)
            .transpose(0, 3, 1, 2, 4, 5)
            .reshape(devices, group_size, prefix_rows, heads // head_count, pair_width)
        )
        incoming = lax.all_to_all(outgoing, ("req", "head"), 0, 0, tiled=True)
        chunks.append(
            incoming.reshape(req_count, head_count, group_size, prefix_rows, heads // head_count, pair_width)
            .transpose(0, 2, 1, 3, 4, 5)
            .reshape(req_count, group_size, head_count * prefix_rows, heads // head_count, pair_width)
        )
    current = chunks[0][0]
    relaid = jnp.stack(chunks, axis=1).reshape((req_count * local_layers,) + chunks[0].shape[1:])
    dealt_acts = jnp.take(stretch_acts, req_order, axis=0)
    dealt_rows = lax.all_to_all(dealt_acts, "req", split_axis=0, concat_axis=1, tiled=True).reshape(
        group_size, req_count, stretch_rows, features
    )
    gathered = lax.all_gather(dealt_rows, "head", axis=2, tiled=True)
    normed = (
        layer_norm(gathered.astype(jnp.float32), attn_gain)
        .astype(jnp.bfloat16)
        .reshape(group_size * stretch_max, features)
    )
    mixed = jnp.dot(
        normed,
        in_weight.reshape(features, heads_here * 3 * head_dim),
        preferred_element_type=jnp.float32,
    )
    mixed = mixed.reshape(group_size, stretch_max, heads_here, 3 * head_dim).astype(jnp.bfloat16)
    contexts = []
    for member in range(group_size):
        pairs = jnp.concatenate([current[member], mixed[member, :, :, head_dim:]], axis=0)
        contexts.append(
            attend(mixed[member, :, :, :head_dim], pairs, member_prefix[member], slopes, head_dim)
        )
    context = jnp.concatenate(contexts, axis=0)
    partial_attn = jnp.dot(
        context,
        out_weight.reshape(heads_here * head_dim, features),
        preferred_element_type=jnp.float32,
    )
    partial_attn = partial_attn.reshape(group_size, req_count, span_rows, features)
    attn_rows = lax.psum_scatter(
        partial_attn.astype(jnp.bfloat16), "head", scatter_dimension=2, tiled=True
    ).astype(jnp.float32)
    residual_rows = dealt_rows.astype(jnp.float32) + attn_rows
    normed_rows = layer_norm(residual_rows, mlp_gain).astype(jnp.bfloat16)
    normed_all = lax.all_gather(normed_rows, "head", axis=2, tiled=True)
    inner = jax.nn.gelu(
        jnp.dot(
            normed_all.reshape(group_size * stretch_max, features),
            up_weight,
            preferred_element_type=jnp.float32,
        ),
        approximate=False,
    ).astype(jnp.bfloat16)
    partial_mlp = jnp.dot(inner, down_weight, preferred_element_type=jnp.float32).reshape(
        group_size, req_count, span_rows, features
    )
    mlp_rows = lax.psum_scatter(
        partial_mlp.astype(jnp.bfloat16), "head", scatter_dimension=2, tiled=True
    ).astype(jnp.float32)
    row_number = (
        jnp.arange(req_count, dtype=jnp.int32)[:, None] * head_count + head_index
    ) * stretch_rows + jnp.arange(stretch_rows, dtype=jnp.int32)[None, :]
    usable = row_number[None] < member_stretch[:, None, None]
    result = jnp.where(
        usable[..., None], residual_rows + mlp_rows, jnp.zeros((), jnp.float32)
    ).astype(jnp.bfloat16)
    returned = lax.all_to_all(result, "req", split_axis=1, concat_axis=0, tiled=True).reshape(
        requests, stretch_rows, features
    )
    inverse = jnp.argsort(req_order)
    layer_out = jnp.take(returned, inverse, axis=0)
    return (layer_out, relaid)


def solution(mesh):
    return jax.shard_map(
        local,
        mesh=mesh,
        in_specs=(
            P(None, ("req", "head"), None),
            P("req", None, "head", None, None),
            P(),
            P(),
            P(),
            P(),
            P(None, "head", None),
            P("head"),
            P("head", None, None),
            P(),
            P(None, "head"),
            P("head", None),
        ),
        out_specs=(P(None, ("req", "head"), None), P(None, "req", None, "head", None)),
        check_vma=False,
    )
```

```python
import math

import jax
import jax.numpy as jnp
from jax import lax
from jax.sharding import PartitionSpec as P

EPSILON = 1e-05


def layer_norm(values, gain):
    average = jnp.mean(values, axis=-1, keepdims=True)
    centred = values - average
    variance = jnp.mean(centred * centred, axis=-1, keepdims=True)
    return centred * lax.rsqrt(variance + EPSILON) * gain.astype(jnp.float32)


def attend(queries, pairs, prefix_len, slopes, head_dim):
    stretch = queries.shape[0]
    prefix = pairs.shape[0] - stretch
    keys_part = pairs[..., :head_dim]
    values_part = pairs[..., head_dim:]
    scores = jnp.einsum("qhd,khd->hqk", queries, keys_part, preferred_element_type=jnp.float32) * (
        1.0 / math.sqrt(head_dim)
    )
    row_index = jnp.arange(stretch, dtype=jnp.int32)
    key_index = jnp.arange(prefix + stretch, dtype=jnp.int32)
    in_prefix = key_index < prefix
    query_pos = prefix_len + row_index
    key_pos = jnp.where(in_prefix, key_index, prefix_len + key_index - prefix)
    allowed = jnp.where(
        in_prefix[None, :],
        key_index[None, :] < prefix_len,
        (key_index - prefix)[None, :] <= row_index[:, None],
    )
    distance = (query_pos[:, None] - key_pos[None, :]).astype(jnp.float32)
    scores = scores - slopes[:, None, None] * distance[None]
    scores = jnp.where(allowed[None], scores, -jnp.inf)
    highest = jnp.max(scores, axis=-1, keepdims=True)
    expo = jnp.exp(scores - highest)
    soft = (expo / jnp.sum(expo, axis=-1, keepdims=True)).astype(jnp.bfloat16)
    context = jnp.einsum("hqk,khd->qhd", soft, values_part, preferred_element_type=jnp.float32)
    return context.astype(jnp.bfloat16).reshape(stretch, -1)


def head_sum(partial, head_count, stretch_rows):
    shape = partial.shape[:2] + (head_count, stretch_rows) + partial.shape[3:]
    pieces = lax.all_to_all(
        partial.astype(jnp.bfloat16).reshape(shape), "head", split_axis=2, concat_axis=2, tiled=True
    )
    return jnp.sum(pieces.astype(jnp.float32), axis=2)


def local(
    stretch_acts,
    cache_prefill,
    stretch_lens,
    prefix_lens,
    req_order,
    attn_gain,
    in_weight,
    slopes,
    out_weight,
    mlp_gain,
    up_weight,
    down_weight,
):
    req_count = lax.axis_size("req")
    head_count = lax.axis_size("head")
    req_index = lax.axis_index("req")
    head_index = lax.axis_index("head")
    requests = stretch_acts.shape[0]
    stretch_rows = stretch_acts.shape[1]
    features = stretch_acts.shape[2]
    group_size = requests // req_count
    span_rows = head_count * stretch_rows
    stretch_max = req_count * span_rows
    prefix_rows = cache_prefill.shape[2]
    heads_here = in_weight.shape[1]
    pair_width = cache_prefill.shape[4]
    head_dim = pair_width // 2
    members = lax.dynamic_slice_in_dim(req_order, req_index * group_size, group_size)
    member_stretch = jnp.take(stretch_lens, members)
    member_prefix = jnp.take(prefix_lens, members)
    ordered_prefix = jnp.take(prefix_lens, req_order)
    positions = head_index * prefix_rows + jnp.arange(prefix_rows, dtype=jnp.int32)
    keep = positions[None, :] < ordered_prefix[:, None]
    local_layers = cache_prefill.shape[0]
    slots = cache_prefill.shape[1]
    heads = cache_prefill.shape[3]
    devices = req_count * head_count
    chunks = []
    for layer in range(local_layers):
        dealt_cache = jnp.where(
            keep[:, :, None, None],
            jnp.take(cache_prefill[layer], req_order, axis=0),
            jnp.zeros((), cache_prefill.dtype),
        )
        outgoing = (
            dealt_cache.reshape(req_count, group_size, prefix_rows, head_count, heads // head_count, pair_width)
            .transpose(0, 3, 1, 2, 4, 5)
            .reshape(devices, group_size, prefix_rows, heads // head_count, pair_width)
        )
        incoming = lax.all_to_all(outgoing, ("req", "head"), 0, 0, tiled=True)
        chunks.append(
            incoming.reshape(req_count, head_count, group_size, prefix_rows, heads // head_count, pair_width)
            .transpose(0, 2, 1, 3, 4, 5)
            .reshape(req_count, group_size, head_count * prefix_rows, heads // head_count, pair_width)
        )
    current = chunks[0][0]
    relaid = jnp.stack(chunks, axis=1).reshape((req_count * local_layers,) + chunks[0].shape[1:])
    dealt_acts = jnp.take(stretch_acts, req_order, axis=0)
    dealt_rows = lax.all_to_all(dealt_acts, "req", split_axis=0, concat_axis=1, tiled=True).reshape(
        group_size, req_count, stretch_rows, features
    )
    gathered = lax.all_gather(dealt_rows, "head", axis=2, tiled=True)
    normed = (
        layer_norm(gathered.astype(jnp.float32), attn_gain)
        .astype(jnp.bfloat16)
        .reshape(group_size * stretch_max, features)
    )
    mixed = jnp.dot(
        normed,
        in_weight.reshape(features, heads_here * 3 * head_dim),
        preferred_element_type=jnp.float32,
    )
    mixed = mixed.reshape(group_size, stretch_max, heads_here, 3 * head_dim).astype(jnp.bfloat16)
    contexts = []
    for member in range(group_size):
        pairs = jnp.concatenate([current[member], mixed[member, :, :, head_dim:]], axis=0)
        contexts.append(
            attend(mixed[member, :, :, :head_dim], pairs, member_prefix[member], slopes, head_dim)
        )
    context = jnp.concatenate(contexts, axis=0)
    partial_attn = jnp.dot(
        context,
        out_weight.reshape(heads_here * head_dim, features),
        preferred_element_type=jnp.float32,
    )
    partial_attn = partial_attn.reshape(group_size, req_count, span_rows, features)
    attn_rows = head_sum(partial_attn, head_count, stretch_rows)
    residual_rows = dealt_rows.astype(jnp.float32) + attn_rows
    normed_rows = layer_norm(residual_rows, mlp_gain).astype(jnp.bfloat16)
    normed_all = lax.all_gather(normed_rows, "head", axis=2, tiled=True)
    inner = jax.nn.gelu(
        jnp.dot(
            normed_all.reshape(group_size * stretch_max, features),
            up_weight,
            preferred_element_type=jnp.float32,
        ),
        approximate=False,
    ).astype(jnp.bfloat16)
    partial_mlp = jnp.dot(inner, down_weight, preferred_element_type=jnp.float32).reshape(
        group_size, req_count, span_rows, features
    )
    mlp_rows = head_sum(partial_mlp, head_count, stretch_rows)
    row_number = (
        jnp.arange(req_count, dtype=jnp.int32)[:, None] * head_count + head_index
    ) * stretch_rows + jnp.arange(stretch_rows, dtype=jnp.int32)[None, :]
    usable = row_number[None] < member_stretch[:, None, None]
    result = jnp.where(
        usable[..., None], residual_rows + mlp_rows, jnp.zeros((), jnp.float32)
    ).astype(jnp.bfloat16)
    returned = lax.all_to_all(result, "req", split_axis=1, concat_axis=0, tiled=True).reshape(
        requests, stretch_rows, features
    )
    inverse = jnp.argsort(req_order)
    layer_out = jnp.take(returned, inverse, axis=0)
    return (layer_out, relaid)


def solution(mesh):
    return jax.shard_map(
        local,
        mesh=mesh,
        in_specs=(
            P(None, ("req", "head"), None),
            P("req", None, "head", None, None),
            P(),
            P(),
            P(),
            P(),
            P(None, "head", None),
            P("head"),
            P("head", None, None),
            P(),
            P(None, "head"),
            P("head", None),
        ),
        out_specs=(P(None, ("req", "head"), None), P(None, "req", None, "head", None)),
        check_vma=False,
    )
```

```python
import math

import jax
import jax.numpy as jnp
from jax import lax
from jax.sharding import PartitionSpec as P

EPSILON = 1e-05


def layer_norm(values, gain):
    average = jnp.mean(values, axis=-1, keepdims=True)
    centred = values - average
    variance = jnp.mean(centred * centred, axis=-1, keepdims=True)
    return centred * lax.rsqrt(variance + EPSILON) * gain.astype(jnp.float32)


def attend(queries, pairs, prefix_len, slopes, head_dim):
    stretch = queries.shape[0]
    prefix = pairs.shape[0] - stretch
    keys_part = pairs[..., :head_dim]
    values_part = pairs[..., head_dim:]
    scores = jnp.einsum("qhd,khd->hqk", queries, keys_part, preferred_element_type=jnp.float32) * (
        1.0 / math.sqrt(head_dim)
    )
    row_index = jnp.arange(stretch, dtype=jnp.int32)
    key_index = jnp.arange(prefix + stretch, dtype=jnp.int32)
    in_prefix = key_index < prefix
    query_pos = prefix_len + row_index
    key_pos = jnp.where(in_prefix, key_index, prefix_len + key_index - prefix)
    allowed = jnp.where(
        in_prefix[None, :],
        key_index[None, :] < prefix_len,
        (key_index - prefix)[None, :] <= row_index[:, None],
    )
    distance = (query_pos[:, None] - key_pos[None, :]).astype(jnp.float32)
    scores = scores - slopes[:, None, None] * distance[None]
    scores = jnp.where(allowed[None], scores, -jnp.inf)
    highest = jnp.max(scores, axis=-1, keepdims=True)
    expo = jnp.exp(scores - highest)
    soft = (expo / jnp.sum(expo, axis=-1, keepdims=True)).astype(jnp.bfloat16)
    context = jnp.einsum("hqk,khd->qhd", soft, values_part, preferred_element_type=jnp.float32)
    return context.astype(jnp.bfloat16).reshape(stretch, -1)


def head_sum(partial, head_count, stretch_rows):
    shape = partial.shape[:2] + (head_count, stretch_rows) + partial.shape[3:]
    pieces = lax.all_to_all(
        partial.astype(jnp.bfloat16).reshape(shape), "head", split_axis=2, concat_axis=2, tiled=True
    )
    return jnp.sum(pieces.astype(jnp.float32), axis=2)


def local(
    stretch_acts,
    cache_prefill,
    stretch_lens,
    prefix_lens,
    req_order,
    attn_gain,
    in_weight,
    slopes,
    out_weight,
    mlp_gain,
    up_weight,
    down_weight,
):
    req_count = lax.axis_size("req")
    head_count = lax.axis_size("head")
    req_index = lax.axis_index("req")
    head_index = lax.axis_index("head")
    requests = stretch_acts.shape[0]
    stretch_rows = stretch_acts.shape[1]
    features = stretch_acts.shape[2]
    group_size = requests // req_count
    span_rows = head_count * stretch_rows
    stretch_max = req_count * span_rows
    prefix_rows = cache_prefill.shape[2]
    heads_here = in_weight.shape[1]
    pair_width = cache_prefill.shape[4]
    head_dim = pair_width // 2
    members = lax.dynamic_slice_in_dim(req_order, req_index * group_size, group_size)
    member_stretch = jnp.take(stretch_lens, members)
    member_prefix = jnp.take(prefix_lens, members)
    ordered_prefix = jnp.take(prefix_lens, req_order)
    positions = head_index * prefix_rows + jnp.arange(prefix_rows, dtype=jnp.int32)
    keep = positions[None, :] < ordered_prefix[:, None]
    local_layers = cache_prefill.shape[0]
    slots = cache_prefill.shape[1]
    heads = cache_prefill.shape[3]
    devices = req_count * head_count
    chunks = []
    for layer in range(local_layers):
        taken = jnp.stack(
            [lax.dynamic_index_in_dim(cache_prefill[layer], req_order[slot], 0, False) for slot in range(slots)]
        )
        dealt_cache = jnp.where(keep[:, :, None, None], taken, jnp.zeros((), cache_prefill.dtype))
        outgoing = (
            dealt_cache.reshape(req_count, group_size, prefix_rows, head_count, heads // head_count, pair_width)
            .transpose(0, 3, 1, 2, 4, 5)
            .reshape(devices, group_size, prefix_rows, heads // head_count, pair_width)
        )
        incoming = lax.all_to_all(outgoing, ("req", "head"), 0, 0, tiled=True)
        chunks.append(
            incoming.reshape(req_count, head_count, group_size, prefix_rows, heads // head_count, pair_width)
            .transpose(0, 2, 1, 3, 4, 5)
            .reshape(req_count, group_size, head_count * prefix_rows, heads // head_count, pair_width)
        )
    current = chunks[0][0]
    relaid = jnp.stack(chunks, axis=1).reshape((req_count * local_layers,) + chunks[0].shape[1:])
    dealt_acts = jnp.take(stretch_acts, req_order, axis=0)
    dealt_rows = lax.all_to_all(dealt_acts, "req", split_axis=0, concat_axis=1, tiled=True).reshape(
        group_size, req_count, stretch_rows, features
    )
    gathered = lax.all_gather(dealt_rows, "head", axis=2, tiled=True)
    normed = (
        layer_norm(gathered.astype(jnp.float32), attn_gain)
        .astype(jnp.bfloat16)
        .reshape(group_size * stretch_max, features)
    )
    mixed = jnp.dot(
        normed,
        in_weight.reshape(features, heads_here * 3 * head_dim),
        preferred_element_type=jnp.float32,
    )
    mixed = mixed.reshape(group_size, stretch_max, heads_here, 3 * head_dim).astype(jnp.bfloat16)
    contexts = []
    for member in range(group_size):
        pairs = jnp.concatenate([current[member], mixed[member, :, :, head_dim:]], axis=0)
        contexts.append(
            attend(mixed[member, :, :, :head_dim], pairs, member_prefix[member], slopes, head_dim)
        )
    context = jnp.concatenate(contexts, axis=0)
    partial_attn = jnp.dot(
        context,
        out_weight.reshape(heads_here * head_dim, features),
        preferred_element_type=jnp.float32,
    )
    partial_attn = partial_attn.reshape(group_size, req_count, span_rows, features)
    attn_rows = head_sum(partial_attn, head_count, stretch_rows)
    residual_rows = dealt_rows.astype(jnp.float32) + attn_rows
    normed_rows = layer_norm(residual_rows, mlp_gain).astype(jnp.bfloat16)
    normed_all = lax.all_gather(normed_rows, "head", axis=2, tiled=True)
    inner = jax.nn.gelu(
        jnp.dot(
            normed_all.reshape(group_size * stretch_max, features),
            up_weight,
            preferred_element_type=jnp.float32,
        ),
        approximate=False,
    ).astype(jnp.bfloat16)
    partial_mlp = jnp.dot(inner, down_weight, preferred_element_type=jnp.float32).reshape(
        group_size, req_count, span_rows, features
    )
    mlp_rows = head_sum(partial_mlp, head_count, stretch_rows)
    row_number = (
        jnp.arange(req_count, dtype=jnp.int32)[:, None] * head_count + head_index
    ) * stretch_rows + jnp.arange(stretch_rows, dtype=jnp.int32)[None, :]
    usable = row_number[None] < member_stretch[:, None, None]
    result = jnp.where(
        usable[..., None], residual_rows + mlp_rows, jnp.zeros((), jnp.float32)
    ).astype(jnp.bfloat16)
    returned = lax.all_to_all(result, "req", split_axis=1, concat_axis=0, tiled=True).reshape(
        requests, stretch_rows, features
    )
    inverse = jnp.argsort(req_order)
    layer_out = jnp.take(returned, inverse, axis=0)
    return (layer_out, relaid)


def solution(mesh):
    return jax.shard_map(
        local,
        mesh=mesh,
        in_specs=(
            P(None, ("req", "head"), None),
            P("req", None, "head", None, None),
            P(),
            P(),
            P(),
            P(),
            P(None, "head", None),
            P("head"),
            P("head", None, None),
            P(),
            P(None, "head"),
            P("head", None),
        ),
        out_specs=(P(None, ("req", "head"), None), P(None, "req", None, "head", None)),
        check_vma=False,
    )
```

```python
import math

import jax
import jax.numpy as jnp
from jax import lax
from jax.sharding import PartitionSpec as P

EPSILON = 1e-05


def layer_norm(values, gain):
    average = jnp.mean(values, axis=-1, keepdims=True)
    centred = values - average
    variance = jnp.mean(centred * centred, axis=-1, keepdims=True)
    return centred * lax.rsqrt(variance + EPSILON) * gain.astype(jnp.float32)


def attend(queries, pairs, prefix_len, slopes, head_dim):
    stretch = queries.shape[0]
    prefix = pairs.shape[0] - stretch
    keys_part = pairs[..., :head_dim]
    values_part = pairs[..., head_dim:]
    scores = jnp.einsum("qhd,khd->hqk", queries, keys_part, preferred_element_type=jnp.float32) * (
        1.0 / math.sqrt(head_dim)
    )
    row_index = jnp.arange(stretch, dtype=jnp.int32)
    key_index = jnp.arange(prefix + stretch, dtype=jnp.int32)
    in_prefix = key_index < prefix
    query_pos = prefix_len + row_index
    key_pos = jnp.where(in_prefix, key_index, prefix_len + key_index - prefix)
    allowed = jnp.where(
        in_prefix[None, :],
        key_index[None, :] < prefix_len,
        (key_index - prefix)[None, :] <= row_index[:, None],
    )
    distance = (query_pos[:, None] - key_pos[None, :]).astype(jnp.float32)
    scores = scores - slopes[:, None, None] * distance[None]
    scores = jnp.where(allowed[None], scores, -jnp.inf)
    highest = jnp.max(scores, axis=-1, keepdims=True)
    expo = jnp.exp(scores - highest)
    soft = (expo / jnp.sum(expo, axis=-1, keepdims=True)).astype(jnp.bfloat16)
    context = jnp.einsum("hqk,khd->qhd", soft, values_part, preferred_element_type=jnp.float32)
    return context.astype(jnp.bfloat16).reshape(stretch, -1)


def head_sum(partial, head_count, stretch_rows):
    shape = partial.shape[:2] + (head_count, stretch_rows) + partial.shape[3:]
    pieces = lax.all_to_all(
        partial.astype(jnp.bfloat16).reshape(shape), "head", split_axis=2, concat_axis=2, tiled=True
    )
    return jnp.sum(pieces.astype(jnp.float32), axis=2)


def local(
    stretch_acts,
    cache_prefill,
    stretch_lens,
    prefix_lens,
    req_order,
    attn_gain,
    in_weight,
    slopes,
    out_weight,
    mlp_gain,
    up_weight,
    down_weight,
):
    req_count = lax.axis_size("req")
    head_count = lax.axis_size("head")
    req_index = lax.axis_index("req")
    head_index = lax.axis_index("head")
    requests = stretch_acts.shape[0]
    stretch_rows = stretch_acts.shape[1]
    features = stretch_acts.shape[2]
    group_size = requests // req_count
    span_rows = head_count * stretch_rows
    stretch_max = req_count * span_rows
    prefix_rows = cache_prefill.shape[2]
    heads_here = in_weight.shape[1]
    pair_width = cache_prefill.shape[4]
    head_dim = pair_width // 2
    members = lax.dynamic_slice_in_dim(req_order, req_index * group_size, group_size)
    member_stretch = jnp.take(stretch_lens, members)
    member_prefix = jnp.take(prefix_lens, members)
    ordered_prefix = jnp.take(prefix_lens, req_order)
    positions = head_index * prefix_rows + jnp.arange(prefix_rows, dtype=jnp.int32)
    keep = positions[None, :] < ordered_prefix[:, None]
    local_layers = cache_prefill.shape[0]
    slots = cache_prefill.shape[1]
    heads = cache_prefill.shape[3]
    devices = req_count * head_count
    chunks = []
    for layer in range(local_layers):
        dealt_cache = jnp.where(
            keep[:, :, None, None],
            jnp.take(cache_prefill[layer], req_order, axis=0),
            jnp.zeros((), cache_prefill.dtype),
        )
        outgoing = (
            dealt_cache.reshape(req_count, group_size, prefix_rows, head_count, heads // head_count, pair_width)
            .transpose(1, 0, 3, 2, 4, 5)
            .reshape(group_size, devices, 1, prefix_rows, heads // head_count, pair_width)
        )
        for member in range(group_size):
            incoming = lax.all_to_all(outgoing[member], ("req", "head"), 0, 0, tiled=True)
            chunks.append(
                incoming.reshape(req_count, head_count * prefix_rows, heads // head_count, pair_width)
            )
    relaid = jnp.stack(chunks, axis=1).reshape(
        (req_count * local_layers, group_size) + chunks[0].shape[1:]
    )
    dealt_acts = jnp.take(stretch_acts, req_order, axis=0)
    dealt_rows = lax.all_to_all(dealt_acts, "req", split_axis=0, concat_axis=1, tiled=True).reshape(
        group_size, req_count, stretch_rows, features
    )
    row_number = (
        jnp.arange(req_count, dtype=jnp.int32)[:, None] * head_count + head_index
    ) * stretch_rows + jnp.arange(stretch_rows, dtype=jnp.int32)[None, :]
    results = []
    for member in range(group_size):
        own_rows = dealt_rows[member]
        gathered = lax.all_gather(own_rows, "head", axis=1, tiled=True)
        normed = layer_norm(gathered.astype(jnp.float32), attn_gain).astype(jnp.bfloat16).reshape(stretch_max, features)
        mixed = jnp.dot(
            normed,
            in_weight.reshape(features, heads_here * 3 * head_dim),
            preferred_element_type=jnp.float32,
        )
        mixed = mixed.reshape(stretch_max, heads_here, 3 * head_dim).astype(jnp.bfloat16)
        pairs = jnp.concatenate([chunks[member][0], mixed[:, :, head_dim:]], axis=0)
        context = attend(mixed[:, :, :head_dim], pairs, member_prefix[member], slopes, head_dim)
        partial_attn = jnp.dot(
            context,
            out_weight.reshape(heads_here * head_dim, features),
            preferred_element_type=jnp.float32,
        )
        attn_rows = head_sum(partial_attn.reshape(1, req_count, span_rows, features), head_count, stretch_rows)[0]
        residual_rows = own_rows.astype(jnp.float32) + attn_rows
        normed_rows = layer_norm(residual_rows, mlp_gain).astype(jnp.bfloat16)
        normed_all = lax.all_gather(normed_rows, "head", axis=1, tiled=True)
        inner = jax.nn.gelu(
            jnp.dot(normed_all.reshape(stretch_max, features), up_weight, preferred_element_type=jnp.float32),
            approximate=False,
        ).astype(jnp.bfloat16)
        partial_mlp = jnp.dot(inner, down_weight, preferred_element_type=jnp.float32)
        mlp_rows = head_sum(partial_mlp.reshape(1, req_count, span_rows, features), head_count, stretch_rows)[0]
        usable = row_number < member_stretch[member]
        results.append(
            jnp.where(usable[..., None], residual_rows + mlp_rows, jnp.zeros((), jnp.float32)).astype(jnp.bfloat16)
        )
    result = jnp.stack(results)
    returned = lax.all_to_all(result, "req", split_axis=1, concat_axis=0, tiled=True).reshape(
        requests, stretch_rows, features
    )
    inverse = jnp.argsort(req_order)
    layer_out = jnp.take(returned, inverse, axis=0)
    return (layer_out, relaid)


def solution(mesh):
    return jax.shard_map(
        local,
        mesh=mesh,
        in_specs=(
            P(None, ("req", "head"), None),
            P("req", None, "head", None, None),
            P(),
            P(),
            P(),
            P(),
            P(None, "head", None),
            P("head"),
            P("head", None, None),
            P(),
            P(None, "head"),
            P("head", None),
        ),
        out_specs=(P(None, ("req", "head"), None), P(None, "req", None, "head", None)),
        check_vma=False,
    )
```

```python
import math

import jax
import jax.numpy as jnp
from jax import lax
from jax.sharding import PartitionSpec as P

EPSILON = 1e-05


def layer_norm(values, gain):
    average = jnp.mean(values, axis=-1, keepdims=True)
    centred = values - average
    variance = jnp.mean(centred * centred, axis=-1, keepdims=True)
    return centred * lax.rsqrt(variance + EPSILON) * gain.astype(jnp.float32)


def attend(queries, pairs, prefix_len, slopes, head_dim):
    stretch = queries.shape[0]
    prefix = pairs.shape[0] - stretch
    keys_part = pairs[..., :head_dim]
    values_part = pairs[..., head_dim:]
    scores = jnp.einsum("qhd,khd->hqk", queries, keys_part, preferred_element_type=jnp.float32) * (
        1.0 / math.sqrt(head_dim)
    )
    row_index = jnp.arange(stretch, dtype=jnp.int32)
    key_index = jnp.arange(prefix + stretch, dtype=jnp.int32)
    in_prefix = key_index < prefix
    query_pos = prefix_len + row_index
    key_pos = jnp.where(in_prefix, key_index, prefix_len + key_index - prefix)
    allowed = jnp.where(
        in_prefix[None, :],
        key_index[None, :] < prefix_len,
        (key_index - prefix)[None, :] <= row_index[:, None],
    )
    distance = (query_pos[:, None] - key_pos[None, :]).astype(jnp.float32)
    scores = scores - slopes[:, None, None] * distance[None]
    scores = jnp.where(allowed[None], scores, -jnp.inf)
    highest = jnp.max(scores, axis=-1, keepdims=True)
    expo = jnp.exp(scores - highest)
    soft = (expo / jnp.sum(expo, axis=-1, keepdims=True)).astype(jnp.bfloat16)
    context = jnp.einsum("hqk,khd->qhd", soft, values_part, preferred_element_type=jnp.float32)
    return context.astype(jnp.bfloat16).reshape(stretch, -1)


def head_sum(partial, head_count, stretch_rows):
    shape = partial.shape[:2] + (head_count, stretch_rows) + partial.shape[3:]
    pieces = lax.all_to_all(
        partial.astype(jnp.bfloat16).reshape(shape), "head", split_axis=2, concat_axis=2, tiled=True
    )
    return jnp.sum(pieces.astype(jnp.float32), axis=2)


def local(
    stretch_acts,
    cache_prefill,
    stretch_lens,
    prefix_lens,
    req_order,
    attn_gain,
    in_weight,
    slopes,
    out_weight,
    mlp_gain,
    up_weight,
    down_weight,
):
    req_count = lax.axis_size("req")
    head_count = lax.axis_size("head")
    req_index = lax.axis_index("req")
    head_index = lax.axis_index("head")
    requests = stretch_acts.shape[0]
    stretch_rows = stretch_acts.shape[1]
    features = stretch_acts.shape[2]
    group_size = requests // req_count
    span_rows = head_count * stretch_rows
    stretch_max = req_count * span_rows
    prefix_rows = cache_prefill.shape[2]
    heads_here = in_weight.shape[1]
    pair_width = cache_prefill.shape[4]
    head_dim = pair_width // 2
    members = lax.dynamic_slice_in_dim(req_order, req_index * group_size, group_size)
    member_stretch = jnp.take(stretch_lens, members)
    member_prefix = jnp.take(prefix_lens, members)
    ordered_prefix = jnp.take(prefix_lens, req_order)
    positions = head_index * prefix_rows + jnp.arange(prefix_rows, dtype=jnp.int32)
    keep = positions[None, :] < ordered_prefix[:, None]
    local_layers = cache_prefill.shape[0]
    slots = cache_prefill.shape[1]
    heads = cache_prefill.shape[3]
    devices = req_count * head_count
    chunks = []
    for layer in range(local_layers):
        dealt_cache = jnp.where(
            keep[:, :, None, None],
            jnp.take(cache_prefill[layer], req_order, axis=0),
            jnp.zeros((), cache_prefill.dtype),
        )
        outgoing = (
            dealt_cache.reshape(req_count, group_size, prefix_rows, head_count, heads // head_count, pair_width)
            .transpose(0, 3, 1, 2, 4, 5)
            .reshape(devices, group_size, prefix_rows, heads // head_count, pair_width)
        )
        incoming = lax.all_to_all(outgoing, ("req", "head"), 0, 0, tiled=True)
        chunks.append(
            incoming.reshape(req_count, head_count, group_size, prefix_rows, heads // head_count, pair_width)
            .transpose(0, 2, 1, 3, 4, 5)
            .reshape(req_count, group_size, head_count * prefix_rows, heads // head_count, pair_width)
        )
    current = chunks[0][0]
    relaid = jnp.stack(chunks, axis=1).reshape((req_count * local_layers,) + chunks[0].shape[1:])
    dealt_acts = jnp.take(stretch_acts, req_order, axis=0)
    dealt_rows = lax.all_to_all(dealt_acts, "req", split_axis=0, concat_axis=1, tiled=True).reshape(
        group_size, req_count, stretch_rows, features
    )
    gathered = lax.all_gather(dealt_rows, "head", axis=2, tiled=True)
    normed = (
        layer_norm(gathered.astype(jnp.float32), attn_gain)
        .astype(jnp.bfloat16)
        .reshape(group_size * stretch_max, features)
    )
    mixed = jnp.dot(
        normed,
        in_weight.reshape(features, heads_here * 3 * head_dim),
        preferred_element_type=jnp.float32,
    )
    mixed = mixed.reshape(group_size, stretch_max, heads_here, 3 * head_dim).astype(jnp.bfloat16)
    contexts = []
    for member in range(group_size):
        pairs = jnp.concatenate([current[member], mixed[member, :, :, head_dim:]], axis=0)
        contexts.append(
            attend(mixed[member, :, :, :head_dim], pairs, member_prefix[member], slopes, head_dim)
        )
    context = jnp.concatenate(contexts, axis=0)
    partial_attn = jnp.dot(
        context,
        out_weight.reshape(heads_here * head_dim, features),
        preferred_element_type=jnp.float32,
    )
    partial_attn = partial_attn.reshape(group_size, req_count, span_rows, features)
    attn_all = lax.psum(partial_attn.astype(jnp.bfloat16), "head").astype(jnp.float32)
    residual_all = gathered.astype(jnp.float32) + attn_all
    normed_all = layer_norm(residual_all, mlp_gain).astype(jnp.bfloat16)
    residual_rows = lax.dynamic_slice_in_dim(residual_all, head_index * stretch_rows, stretch_rows, axis=2)
    inner = jax.nn.gelu(
        jnp.dot(
            normed_all.reshape(group_size * stretch_max, features),
            up_weight,
            preferred_element_type=jnp.float32,
        ),
        approximate=False,
    ).astype(jnp.bfloat16)
    partial_mlp = jnp.dot(inner, down_weight, preferred_element_type=jnp.float32).reshape(
        group_size, req_count, span_rows, features
    )
    mlp_rows = head_sum(partial_mlp, head_count, stretch_rows)
    relaid, mlp_rows = lax.optimization_barrier((relaid, mlp_rows))
    row_number = (
        jnp.arange(req_count, dtype=jnp.int32)[:, None] * head_count + head_index
    ) * stretch_rows + jnp.arange(stretch_rows, dtype=jnp.int32)[None, :]
    usable = row_number[None] < member_stretch[:, None, None]
    result = jnp.where(
        usable[..., None], residual_rows + mlp_rows, jnp.zeros((), jnp.float32)
    ).astype(jnp.bfloat16)
    returned = lax.all_to_all(result, "req", split_axis=1, concat_axis=0, tiled=True).reshape(
        requests, stretch_rows, features
    )
    inverse = jnp.argsort(req_order)
    layer_out = jnp.take(returned, inverse, axis=0)
    return (layer_out, relaid)


def solution(mesh):
    return jax.shard_map(
        local,
        mesh=mesh,
        in_specs=(
            P(None, ("req", "head"), None),
            P("req", None, "head", None, None),
            P(),
            P(),
            P(),
            P(),
            P(None, "head", None),
            P("head"),
            P("head", None, None),
            P(),
            P(None, "head"),
            P("head", None),
        ),
        out_specs=(P(None, ("req", "head"), None), P(None, "req", None, "head", None)),
        check_vma=False,
    )
```

```python
import math

import jax
import jax.numpy as jnp
from jax import lax
from jax.sharding import PartitionSpec as P

EPSILON = 1e-05


def layer_norm(values, gain):
    average = jnp.mean(values, axis=-1, keepdims=True)
    centred = values - average
    variance = jnp.mean(centred * centred, axis=-1, keepdims=True)
    return centred * lax.rsqrt(variance + EPSILON) * gain.astype(jnp.float32)


def attend(queries, pairs, prefix_len, slopes, head_dim):
    stretch = queries.shape[0]
    prefix = pairs.shape[0] - stretch
    keys_part = pairs[..., :head_dim]
    values_part = pairs[..., head_dim:]
    scores = jnp.einsum("qhd,khd->hqk", queries, keys_part, preferred_element_type=jnp.float32) * (
        1.0 / math.sqrt(head_dim)
    )
    row_index = jnp.arange(stretch, dtype=jnp.int32)
    key_index = jnp.arange(prefix + stretch, dtype=jnp.int32)
    in_prefix = key_index < prefix
    query_pos = prefix_len + row_index
    key_pos = jnp.where(in_prefix, key_index, prefix_len + key_index - prefix)
    allowed = jnp.where(
        in_prefix[None, :],
        key_index[None, :] < prefix_len,
        (key_index - prefix)[None, :] <= row_index[:, None],
    )
    distance = (query_pos[:, None] - key_pos[None, :]).astype(jnp.float32)
    scores = scores - slopes[:, None, None] * distance[None]
    scores = jnp.where(allowed[None], scores, -jnp.inf)
    highest = jnp.max(scores, axis=-1, keepdims=True)
    expo = jnp.exp(scores - highest)
    soft = (expo / jnp.sum(expo, axis=-1, keepdims=True)).astype(jnp.bfloat16)
    context = jnp.einsum("hqk,khd->qhd", soft, values_part, preferred_element_type=jnp.float32)
    return context.astype(jnp.bfloat16).reshape(stretch, -1)


def head_sum(partial, head_count, stretch_rows):
    shape = partial.shape[:2] + (head_count, stretch_rows) + partial.shape[3:]
    pieces = lax.all_to_all(
        partial.astype(jnp.bfloat16).reshape(shape), "head", split_axis=2, concat_axis=2, tiled=True
    )
    return jnp.sum(pieces.astype(jnp.float32), axis=2)


def local(
    stretch_acts,
    cache_prefill,
    stretch_lens,
    prefix_lens,
    req_order,
    attn_gain,
    in_weight,
    slopes,
    out_weight,
    mlp_gain,
    up_weight,
    down_weight,
):
    req_count = lax.axis_size("req")
    head_count = lax.axis_size("head")
    req_index = lax.axis_index("req")
    head_index = lax.axis_index("head")
    requests = stretch_acts.shape[0]
    stretch_rows = stretch_acts.shape[1]
    features = stretch_acts.shape[2]
    group_size = requests // req_count
    span_rows = head_count * stretch_rows
    stretch_max = req_count * span_rows
    prefix_rows = cache_prefill.shape[2]
    heads_here = in_weight.shape[1]
    pair_width = cache_prefill.shape[4]
    head_dim = pair_width // 2
    members = lax.dynamic_slice_in_dim(req_order, req_index * group_size, group_size)
    member_stretch = jnp.take(stretch_lens, members)
    member_prefix = jnp.take(prefix_lens, members)
    ordered_prefix = jnp.take(prefix_lens, req_order)
    positions = head_index * prefix_rows + jnp.arange(prefix_rows, dtype=jnp.int32)
    keep = positions[None, :] < ordered_prefix[:, None]
    local_layers = cache_prefill.shape[0]
    slots = cache_prefill.shape[1]
    heads = cache_prefill.shape[3]
    devices = req_count * head_count
    chunks = []
    dealt_acts = jnp.take(stretch_acts, req_order, axis=0)
    later_layers = cache_prefill[1:]
    for layer in range(local_layers):
        source = cache_prefill[0] if layer == 0 else later_layers[layer - 1]
        dealt_cache = jnp.where(
            keep[:, :, None, None],
            jnp.take(source, req_order, axis=0),
            jnp.zeros((), cache_prefill.dtype),
        )
        outgoing = (
            dealt_cache.reshape(req_count, group_size, prefix_rows, head_count, heads // head_count, pair_width)
            .transpose(0, 3, 1, 2, 4, 5)
            .reshape(devices, group_size, prefix_rows, heads // head_count, pair_width)
        )
        if layer == 0:
            outgoing, dealt_acts = lax.optimization_barrier((outgoing, dealt_acts))
        incoming = lax.all_to_all(outgoing, ("req", "head"), 0, 0, tiled=True)
        if layer == 0:
            incoming, later_layers = lax.optimization_barrier((incoming, later_layers))
        chunks.append(
            incoming.reshape(req_count, head_count, group_size, prefix_rows, heads // head_count, pair_width)
            .transpose(0, 2, 1, 3, 4, 5)
            .reshape(req_count, group_size, head_count * prefix_rows, heads // head_count, pair_width)
        )
    current = chunks[0][0]
    relaid = jnp.stack(chunks, axis=1).reshape((req_count * local_layers,) + chunks[0].shape[1:])
    dealt_rows = lax.all_to_all(dealt_acts, "req", split_axis=0, concat_axis=1, tiled=True).reshape(
        group_size, req_count, stretch_rows, features
    )
    gathered = lax.all_gather(dealt_rows, "head", axis=2, tiled=True)
    normed = (
        layer_norm(gathered.astype(jnp.float32), attn_gain)
        .astype(jnp.bfloat16)
        .reshape(group_size * stretch_max, features)
    )
    mixed = jnp.dot(
        normed,
        in_weight.reshape(features, heads_here * 3 * head_dim),
        preferred_element_type=jnp.float32,
    )
    mixed = mixed.reshape(group_size, stretch_max, heads_here, 3 * head_dim).astype(jnp.bfloat16)
    contexts = []
    for member in range(group_size):
        pairs = jnp.concatenate([current[member], mixed[member, :, :, head_dim:]], axis=0)
        contexts.append(
            attend(mixed[member, :, :, :head_dim], pairs, member_prefix[member], slopes, head_dim)
        )
    context = jnp.concatenate(contexts, axis=0)
    partial_attn = jnp.dot(
        context,
        out_weight.reshape(heads_here * head_dim, features),
        preferred_element_type=jnp.float32,
    )
    partial_attn = partial_attn.reshape(group_size, req_count, span_rows, features)
    attn_rows = head_sum(partial_attn, head_count, stretch_rows)
    residual_rows = dealt_rows.astype(jnp.float32) + attn_rows
    normed_rows = layer_norm(residual_rows, mlp_gain).astype(jnp.bfloat16)
    normed_all = lax.all_gather(normed_rows, "head", axis=2, tiled=True)
    inner = jax.nn.gelu(
        jnp.dot(
            normed_all.reshape(group_size * stretch_max, features),
            up_weight,
            preferred_element_type=jnp.float32,
        ),
        approximate=False,
    ).astype(jnp.bfloat16)
    partial_mlp = jnp.dot(inner, down_weight, preferred_element_type=jnp.float32).reshape(
        group_size, req_count, span_rows, features
    )
    mlp_rows = head_sum(partial_mlp, head_count, stretch_rows)
    relaid, mlp_rows = lax.optimization_barrier((relaid, mlp_rows))
    row_number = (
        jnp.arange(req_count, dtype=jnp.int32)[:, None] * head_count + head_index
    ) * stretch_rows + jnp.arange(stretch_rows, dtype=jnp.int32)[None, :]
    usable = row_number[None] < member_stretch[:, None, None]
    result = jnp.where(
        usable[..., None], residual_rows + mlp_rows, jnp.zeros((), jnp.float32)
    ).astype(jnp.bfloat16)
    returned = lax.all_to_all(result, "req", split_axis=1, concat_axis=0, tiled=True).reshape(
        requests, stretch_rows, features
    )
    inverse = jnp.argsort(req_order)
    layer_out = jnp.take(returned, inverse, axis=0)
    return (layer_out, relaid)


def solution(mesh):
    return jax.shard_map(
        local,
        mesh=mesh,
        in_specs=(
            P(None, ("req", "head"), None),
            P("req", None, "head", None, None),
            P(),
            P(),
            P(),
            P(),
            P(None, "head", None),
            P("head"),
            P("head", None, None),
            P(),
            P(None, "head"),
            P("head", None),
        ),
        out_specs=(P(None, ("req", "head"), None), P(None, "req", None, "head", None)),
        check_vma=False,
    )
```

```python
import math

import jax
import jax.numpy as jnp
from jax import lax
from jax.sharding import PartitionSpec as P

EPSILON = 1e-05


def layer_norm(values, gain):
    average = jnp.mean(values, axis=-1, keepdims=True)
    centred = values - average
    variance = jnp.mean(centred * centred, axis=-1, keepdims=True)
    return centred * lax.rsqrt(variance + EPSILON) * gain.astype(jnp.float32)


def attend(queries, pairs, prefix_len, slopes, head_dim):
    stretch = queries.shape[0]
    prefix = pairs.shape[0] - stretch
    keys_part = pairs[..., :head_dim]
    values_part = pairs[..., head_dim:]
    scores = jnp.einsum("qhd,khd->hqk", queries, keys_part, preferred_element_type=jnp.float32) * (
        1.0 / math.sqrt(head_dim)
    )
    row_index = jnp.arange(stretch, dtype=jnp.int32)
    key_index = jnp.arange(prefix + stretch, dtype=jnp.int32)
    in_prefix = key_index < prefix
    query_pos = prefix_len + row_index
    key_pos = jnp.where(in_prefix, key_index, prefix_len + key_index - prefix)
    allowed = jnp.where(
        in_prefix[None, :],
        key_index[None, :] < prefix_len,
        (key_index - prefix)[None, :] <= row_index[:, None],
    )
    distance = (query_pos[:, None] - key_pos[None, :]).astype(jnp.float32)
    scores = scores - slopes[:, None, None] * distance[None]
    scores = jnp.where(allowed[None], scores, -jnp.inf)
    highest = jnp.max(scores, axis=-1, keepdims=True)
    expo = jnp.exp(scores - highest)
    soft = (expo / jnp.sum(expo, axis=-1, keepdims=True)).astype(jnp.bfloat16)
    context = jnp.einsum("hqk,khd->qhd", soft, values_part, preferred_element_type=jnp.float32)
    return context.astype(jnp.bfloat16).reshape(stretch, -1)


def head_sum(partial, head_count, stretch_rows):
    inner_size = 4 if head_count % 4 == 0 else head_count
    outer_size = head_count // inner_size
    me = lax.axis_index("head")
    outer_me, inner_me = me // inner_size, me % inner_size
    blocks = partial.astype(jnp.bfloat16).reshape(
        partial.shape[:2] + (outer_size, inner_size, stretch_rows) + partial.shape[3:]
    )
    level_one = lax.dynamic_index_in_dim(blocks, inner_me, 3, False).astype(jnp.float32)
    for shift in range(1, inner_size):
        pairs = [(j, (j // inner_size) * inner_size + (j % inner_size + shift) % inner_size) for j in range(head_count)]
        sent = lax.dynamic_index_in_dim(blocks, (inner_me + shift) % inner_size, 3, False)
        level_one = level_one + lax.ppermute(sent, "head", pairs).astype(jnp.float32)
    rounded_one = level_one.astype(jnp.bfloat16)
    total = lax.dynamic_index_in_dim(level_one, outer_me, 2, False)
    for shift in range(1, outer_size):
        pairs = [(j, ((j // inner_size + shift) % outer_size) * inner_size + j % inner_size) for j in range(head_count)]
        sent = lax.dynamic_index_in_dim(rounded_one, (outer_me + shift) % outer_size, 2, False)
        total = total + lax.ppermute(sent, "head", pairs).astype(jnp.float32)
    return total


def local(
    stretch_acts,
    cache_prefill,
    stretch_lens,
    prefix_lens,
    req_order,
    attn_gain,
    in_weight,
    slopes,
    out_weight,
    mlp_gain,
    up_weight,
    down_weight,
):
    req_count = lax.axis_size("req")
    head_count = lax.axis_size("head")
    req_index = lax.axis_index("req")
    head_index = lax.axis_index("head")
    requests = stretch_acts.shape[0]
    stretch_rows = stretch_acts.shape[1]
    features = stretch_acts.shape[2]
    group_size = requests // req_count
    span_rows = head_count * stretch_rows
    stretch_max = req_count * span_rows
    prefix_rows = cache_prefill.shape[2]
    heads_here = in_weight.shape[1]
    pair_width = cache_prefill.shape[4]
    head_dim = pair_width // 2
    members = lax.dynamic_slice_in_dim(req_order, req_index * group_size, group_size)
    member_stretch = jnp.take(stretch_lens, members)
    member_prefix = jnp.take(prefix_lens, members)
    ordered_prefix = jnp.take(prefix_lens, req_order)
    positions = head_index * prefix_rows + jnp.arange(prefix_rows, dtype=jnp.int32)
    keep = positions[None, :] < ordered_prefix[:, None]
    local_layers = cache_prefill.shape[0]
    slots = cache_prefill.shape[1]
    heads = cache_prefill.shape[3]
    devices = req_count * head_count
    chunks = []
    for layer in range(local_layers):
        dealt_cache = jnp.where(
            keep[:, :, None, None],
            jnp.take(cache_prefill[layer], req_order, axis=0),
            jnp.zeros((), cache_prefill.dtype),
        )
        outgoing = (
            dealt_cache.reshape(req_count, group_size, prefix_rows, head_count, heads // head_count, pair_width)
            .transpose(0, 3, 1, 2, 4, 5)
            .reshape(devices, group_size, prefix_rows, heads // head_count, pair_width)
        )
        incoming = lax.all_to_all(outgoing, ("req", "head"), 0, 0, tiled=True)
        chunks.append(
            incoming.reshape(req_count, head_count, group_size, prefix_rows, heads // head_count, pair_width)
            .transpose(0, 2, 1, 3, 4, 5)
            .reshape(req_count, group_size, head_count * prefix_rows, heads // head_count, pair_width)
        )
    current = chunks[0][0]
    relaid = jnp.stack(chunks, axis=1).reshape((req_count * local_layers,) + chunks[0].shape[1:])
    dealt_acts = jnp.take(stretch_acts, req_order, axis=0)
    dealt_rows = lax.all_to_all(dealt_acts, "req", split_axis=0, concat_axis=1, tiled=True).reshape(
        group_size, req_count, stretch_rows, features
    )
    gathered = lax.all_gather(dealt_rows, "head", axis=2, tiled=True)
    normed = (
        layer_norm(gathered.astype(jnp.float32), attn_gain)
        .astype(jnp.bfloat16)
        .reshape(group_size * stretch_max, features)
    )
    mixed = jnp.dot(
        normed,
        in_weight.reshape(features, heads_here * 3 * head_dim),
        preferred_element_type=jnp.float32,
    )
    mixed = mixed.reshape(group_size, stretch_max, heads_here, 3 * head_dim).astype(jnp.bfloat16)
    contexts = []
    for member in range(group_size):
        pairs = jnp.concatenate([current[member], mixed[member, :, :, head_dim:]], axis=0)
        contexts.append(
            attend(mixed[member, :, :, :head_dim], pairs, member_prefix[member], slopes, head_dim)
        )
    context = jnp.concatenate(contexts, axis=0)
    partial_attn = jnp.dot(
        context,
        out_weight.reshape(heads_here * head_dim, features),
        preferred_element_type=jnp.float32,
    )
    partial_attn = partial_attn.reshape(group_size, req_count, span_rows, features)
    attn_rows = head_sum(partial_attn, head_count, stretch_rows)
    residual_rows = dealt_rows.astype(jnp.float32) + attn_rows
    normed_rows = layer_norm(residual_rows, mlp_gain).astype(jnp.bfloat16)
    normed_all = lax.all_gather(normed_rows, "head", axis=2, tiled=True)
    inner = jax.nn.gelu(
        jnp.dot(
            normed_all.reshape(group_size * stretch_max, features),
            up_weight,
            preferred_element_type=jnp.float32,
        ),
        approximate=False,
    ).astype(jnp.bfloat16)
    partial_mlp = jnp.dot(inner, down_weight, preferred_element_type=jnp.float32).reshape(
        group_size, req_count, span_rows, features
    )
    mlp_rows = head_sum(partial_mlp, head_count, stretch_rows)
    relaid, mlp_rows = lax.optimization_barrier((relaid, mlp_rows))
    row_number = (
        jnp.arange(req_count, dtype=jnp.int32)[:, None] * head_count + head_index
    ) * stretch_rows + jnp.arange(stretch_rows, dtype=jnp.int32)[None, :]
    usable = row_number[None] < member_stretch[:, None, None]
    result = jnp.where(
        usable[..., None], residual_rows + mlp_rows, jnp.zeros((), jnp.float32)
    ).astype(jnp.bfloat16)
    returned = lax.all_to_all(result, "req", split_axis=1, concat_axis=0, tiled=True).reshape(
        requests, stretch_rows, features
    )
    inverse = jnp.argsort(req_order)
    layer_out = jnp.take(returned, inverse, axis=0)
    return (layer_out, relaid)


def solution(mesh):
    return jax.shard_map(
        local,
        mesh=mesh,
        in_specs=(
            P(None, ("req", "head"), None),
            P("req", None, "head", None, None),
            P(),
            P(),
            P(),
            P(),
            P(None, "head", None),
            P("head"),
            P("head", None, None),
            P(),
            P(None, "head"),
            P("head", None),
        ),
        out_specs=(P(None, ("req", "head"), None), P(None, "req", None, "head", None)),
        check_vma=False,
    )
```

```python
import math

import jax
import jax.numpy as jnp
from jax import lax
from jax.sharding import PartitionSpec as P

EPSILON = 1e-05


def layer_norm(values, gain):
    average = jnp.mean(values, axis=-1, keepdims=True)
    centred = values - average
    variance = jnp.mean(centred * centred, axis=-1, keepdims=True)
    return centred * lax.rsqrt(variance + EPSILON) * gain.astype(jnp.float32)


def attend(queries, pairs, prefix_len, slopes, head_dim):
    stretch = queries.shape[0]
    prefix = pairs.shape[0] - stretch
    keys_part = pairs[..., :head_dim]
    values_part = pairs[..., head_dim:]
    scores = jnp.einsum("qhd,khd->hqk", queries, keys_part, preferred_element_type=jnp.float32) * (
        1.0 / math.sqrt(head_dim)
    )
    row_index = jnp.arange(stretch, dtype=jnp.int32)
    key_index = jnp.arange(prefix + stretch, dtype=jnp.int32)
    in_prefix = key_index < prefix
    query_pos = prefix_len + row_index
    key_pos = jnp.where(in_prefix, key_index, prefix_len + key_index - prefix)
    allowed = jnp.where(
        in_prefix[None, :],
        key_index[None, :] < prefix_len,
        (key_index - prefix)[None, :] <= row_index[:, None],
    )
    distance = (query_pos[:, None] - key_pos[None, :]).astype(jnp.float32)
    scores = scores - slopes[:, None, None] * distance[None]
    scores = jnp.where(allowed[None], scores, -jnp.inf)
    highest = jnp.max(scores, axis=-1, keepdims=True)
    expo = jnp.exp(scores - highest)
    soft = (expo / jnp.sum(expo, axis=-1, keepdims=True)).astype(jnp.bfloat16)
    context = jnp.einsum("hqk,khd->qhd", soft, values_part, preferred_element_type=jnp.float32)
    return context.astype(jnp.bfloat16).reshape(stretch, -1)


def head_sum(partial, head_count, stretch_rows):
    inner_size = 4 if head_count % 4 == 0 else head_count
    outer_size = head_count // inner_size
    me = lax.axis_index("head")
    outer_me, inner_me = me // inner_size, me % inner_size
    blocks = partial.astype(jnp.bfloat16).reshape(
        partial.shape[:2] + (outer_size, inner_size, stretch_rows) + partial.shape[3:]
    )
    level_one = lax.dynamic_index_in_dim(blocks, inner_me, 3, False).astype(jnp.float32)
    for shift in range(1, inner_size):
        pairs = [(j, (j // inner_size) * inner_size + (j % inner_size + shift) % inner_size) for j in range(head_count)]
        sent = lax.dynamic_index_in_dim(blocks, (inner_me + shift) % inner_size, 3, False)
        level_one = level_one + lax.ppermute(sent, "head", pairs).astype(jnp.float32)
    rounded_one = level_one.astype(jnp.bfloat16)
    total = lax.dynamic_index_in_dim(level_one, outer_me, 2, False)
    for shift in range(1, outer_size):
        pairs = [(j, ((j // inner_size + shift) % outer_size) * inner_size + j % inner_size) for j in range(head_count)]
        sent = lax.dynamic_index_in_dim(rounded_one, (outer_me + shift) % outer_size, 2, False)
        total = total + lax.ppermute(sent, "head", pairs).astype(jnp.float32)
    return total


def head_gather(rows, head_count):
    inner_size = 4 if head_count % 4 == 0 else head_count
    outer_size = head_count // inner_size
    me = lax.axis_index("head")
    outer_me, inner_me = me // inner_size, me % inner_size
    held = [rows]
    for shift in range(1, outer_size):
        pairs = [(j, ((j // inner_size + shift) % outer_size) * inner_size + j % inner_size) for j in range(head_count)]
        held.append(lax.ppermute(rows, "head", pairs))
    by_outer = jnp.take(jnp.stack(held), (outer_me - jnp.arange(outer_size)) % outer_size, axis=0)
    held = [by_outer]
    for shift in range(1, inner_size):
        pairs = [(j, (j // inner_size) * inner_size + (j % inner_size + shift) % inner_size) for j in range(head_count)]
        held.append(lax.ppermute(by_outer, "head", pairs))
    by_inner = jnp.take(jnp.stack(held), (inner_me - jnp.arange(inner_size)) % inner_size, axis=0)
    gathered = jnp.moveaxis(by_inner, (0, 1), (3, 2))
    return gathered.reshape(rows.shape[:2] + (head_count * rows.shape[2],) + rows.shape[3:])


def local(
    stretch_acts,
    cache_prefill,
    stretch_lens,
    prefix_lens,
    req_order,
    attn_gain,
    in_weight,
    slopes,
    out_weight,
    mlp_gain,
    up_weight,
    down_weight,
):
    req_count = lax.axis_size("req")
    head_count = lax.axis_size("head")
    req_index = lax.axis_index("req")
    head_index = lax.axis_index("head")
    requests = stretch_acts.shape[0]
    stretch_rows = stretch_acts.shape[1]
    features = stretch_acts.shape[2]
    group_size = requests // req_count
    span_rows = head_count * stretch_rows
    stretch_max = req_count * span_rows
    prefix_rows = cache_prefill.shape[2]
    heads_here = in_weight.shape[1]
    pair_width = cache_prefill.shape[4]
    head_dim = pair_width // 2
    members = lax.dynamic_slice_in_dim(req_order, req_index * group_size, group_size)
    member_stretch = jnp.take(stretch_lens, members)
    member_prefix = jnp.take(prefix_lens, members)
    ordered_prefix = jnp.take(prefix_lens, req_order)
    positions = head_index * prefix_rows + jnp.arange(prefix_rows, dtype=jnp.int32)
    keep = positions[None, :] < ordered_prefix[:, None]
    local_layers = cache_prefill.shape[0]
    slots = cache_prefill.shape[1]
    heads = cache_prefill.shape[3]
    devices = req_count * head_count
    chunks = []
    for layer in range(local_layers):
        dealt_cache = jnp.where(
            keep[:, :, None, None],
            jnp.take(cache_prefill[layer], req_order, axis=0),
            jnp.zeros((), cache_prefill.dtype),
        )
        outgoing = (
            dealt_cache.reshape(req_count, group_size, prefix_rows, head_count, heads // head_count, pair_width)
            .transpose(0, 3, 1, 2, 4, 5)
            .reshape(devices, group_size, prefix_rows, heads // head_count, pair_width)
        )
        incoming = lax.all_to_all(outgoing, ("req", "head"), 0, 0, tiled=True)
        chunks.append(
            incoming.reshape(req_count, head_count, group_size, prefix_rows, heads // head_count, pair_width)
            .transpose(0, 2, 1, 3, 4, 5)
            .reshape(req_count, group_size, head_count * prefix_rows, heads // head_count, pair_width)
        )
    current = chunks[0][0]
    relaid = jnp.stack(chunks, axis=1).reshape((req_count * local_layers,) + chunks[0].shape[1:])
    dealt_acts = jnp.take(stretch_acts, req_order, axis=0)
    dealt_rows = lax.all_to_all(dealt_acts, "req", split_axis=0, concat_axis=1, tiled=True).reshape(
        group_size, req_count, stretch_rows, features
    )
    gathered = head_gather(dealt_rows, head_count)
    normed = (
        layer_norm(gathered.astype(jnp.float32), attn_gain)
        .astype(jnp.bfloat16)
        .reshape(group_size * stretch_max, features)
    )
    mixed = jnp.dot(
        normed,
        in_weight.reshape(features, heads_here * 3 * head_dim),
        preferred_element_type=jnp.float32,
    )
    mixed = mixed.reshape(group_size, stretch_max, heads_here, 3 * head_dim).astype(jnp.bfloat16)
    contexts = []
    for member in range(group_size):
        pairs = jnp.concatenate([current[member], mixed[member, :, :, head_dim:]], axis=0)
        contexts.append(
            attend(mixed[member, :, :, :head_dim], pairs, member_prefix[member], slopes, head_dim)
        )
    context = jnp.concatenate(contexts, axis=0)
    partial_attn = jnp.dot(
        context,
        out_weight.reshape(heads_here * head_dim, features),
        preferred_element_type=jnp.float32,
    )
    partial_attn = partial_attn.reshape(group_size, req_count, span_rows, features)
    attn_rows = head_sum(partial_attn, head_count, stretch_rows)
    residual_rows = dealt_rows.astype(jnp.float32) + attn_rows
    normed_rows = layer_norm(residual_rows, mlp_gain).astype(jnp.bfloat16)
    normed_all = head_gather(normed_rows, head_count)
    inner = jax.nn.gelu(
        jnp.dot(
            normed_all.reshape(group_size * stretch_max, features),
            up_weight,
            preferred_element_type=jnp.float32,
        ),
        approximate=False,
    ).astype(jnp.bfloat16)
    partial_mlp = jnp.dot(inner, down_weight, preferred_element_type=jnp.float32).reshape(
        group_size, req_count, span_rows, features
    )
    mlp_rows = head_sum(partial_mlp, head_count, stretch_rows)
    relaid, mlp_rows = lax.optimization_barrier((relaid, mlp_rows))
    row_number = (
        jnp.arange(req_count, dtype=jnp.int32)[:, None] * head_count + head_index
    ) * stretch_rows + jnp.arange(stretch_rows, dtype=jnp.int32)[None, :]
    usable = row_number[None] < member_stretch[:, None, None]
    result = jnp.where(
        usable[..., None], residual_rows + mlp_rows, jnp.zeros((), jnp.float32)
    ).astype(jnp.bfloat16)
    returned = lax.all_to_all(result, "req", split_axis=1, concat_axis=0, tiled=True).reshape(
        requests, stretch_rows, features
    )
    inverse = jnp.argsort(req_order)
    layer_out = jnp.take(returned, inverse, axis=0)
    return (layer_out, relaid)


def solution(mesh):
    return jax.shard_map(
        local,
        mesh=mesh,
        in_specs=(
            P(None, ("req", "head"), None),
            P("req", None, "head", None, None),
            P(),
            P(),
            P(),
            P(),
            P(None, "head", None),
            P("head"),
            P("head", None, None),
            P(),
            P(None, "head"),
            P("head", None),
        ),
        out_specs=(P(None, ("req", "head"), None), P(None, "req", None, "head", None)),
        check_vma=False,
    )
```

```python
import math

import jax
import jax.numpy as jnp
from jax import lax
from jax.sharding import PartitionSpec as P

EPSILON = 1e-05


def layer_norm(values, gain):
    average = jnp.mean(values, axis=-1, keepdims=True)
    centred = values - average
    variance = jnp.mean(centred * centred, axis=-1, keepdims=True)
    return centred * lax.rsqrt(variance + EPSILON) * gain.astype(jnp.float32)


def attend(queries, pairs, prefix_len, slopes, head_dim):
    stretch = queries.shape[0]
    prefix = pairs.shape[0] - stretch
    keys_part = pairs[..., :head_dim]
    values_part = pairs[..., head_dim:]
    scores = jnp.einsum("qhd,khd->hqk", queries, keys_part, preferred_element_type=jnp.float32) * (
        1.0 / math.sqrt(head_dim)
    )
    row_index = jnp.arange(stretch, dtype=jnp.int32)
    key_index = jnp.arange(prefix + stretch, dtype=jnp.int32)
    in_prefix = key_index < prefix
    query_pos = prefix_len + row_index
    key_pos = jnp.where(in_prefix, key_index, prefix_len + key_index - prefix)
    allowed = jnp.where(
        in_prefix[None, :],
        key_index[None, :] < prefix_len,
        (key_index - prefix)[None, :] <= row_index[:, None],
    )
    distance = (query_pos[:, None] - key_pos[None, :]).astype(jnp.float32)
    scores = scores - slopes[:, None, None] * distance[None]
    scores = jnp.where(allowed[None], scores, -jnp.inf)
    highest = jnp.max(scores, axis=-1, keepdims=True)
    expo = jnp.exp(scores - highest)
    soft = (expo / jnp.sum(expo, axis=-1, keepdims=True)).astype(jnp.bfloat16)
    context = jnp.einsum("hqk,khd->qhd", soft, values_part, preferred_element_type=jnp.float32)
    return context.astype(jnp.bfloat16).reshape(stretch, -1)


def head_sum(partial, head_count, stretch_rows):
    inner_size = 4 if head_count % 4 == 0 else head_count
    outer_size = head_count // inner_size
    me = lax.axis_index("head")
    outer_me, inner_me = me // inner_size, me % inner_size
    blocks = partial.astype(jnp.bfloat16).reshape(
        partial.shape[:2] + (outer_size, inner_size, stretch_rows) + partial.shape[3:]
    )
    level_one = lax.dynamic_index_in_dim(blocks, inner_me, 3, False).astype(jnp.float32)
    for shift in range(1, inner_size):
        pairs = [(j, (j // inner_size) * inner_size + (j % inner_size + shift) % inner_size) for j in range(head_count)]
        sent = lax.dynamic_index_in_dim(blocks, (inner_me + shift) % inner_size, 3, False)
        level_one = level_one + lax.ppermute(sent, "head", pairs).astype(jnp.float32)
    rounded_one = level_one.astype(jnp.bfloat16)
    total = lax.dynamic_index_in_dim(level_one, outer_me, 2, False)
    for shift in range(1, outer_size):
        pairs = [(j, ((j // inner_size + shift) % outer_size) * inner_size + j % inner_size) for j in range(head_count)]
        sent = lax.dynamic_index_in_dim(rounded_one, (outer_me + shift) % outer_size, 2, False)
        total = total + lax.ppermute(sent, "head", pairs).astype(jnp.float32)
    return total


def land(incoming, req_count, head_count):
    shape = (req_count, head_count) + incoming.shape[1:]
    landed = incoming.reshape(shape).transpose(0, 2, 1, 3, 4, 5)
    return landed.reshape(landed.shape[:2] + (-1,) + landed.shape[4:])


def local(
    stretch_acts,
    cache_prefill,
    stretch_lens,
    prefix_lens,
    req_order,
    attn_gain,
    in_weight,
    slopes,
    out_weight,
    mlp_gain,
    up_weight,
    down_weight,
):
    req_count = lax.axis_size("req")
    head_count = lax.axis_size("head")
    req_index = lax.axis_index("req")
    head_index = lax.axis_index("head")
    requests = stretch_acts.shape[0]
    stretch_rows = stretch_acts.shape[1]
    features = stretch_acts.shape[2]
    group_size = requests // req_count
    span_rows = head_count * stretch_rows
    stretch_max = req_count * span_rows
    prefix_rows = cache_prefill.shape[2]
    heads_here = in_weight.shape[1]
    pair_width = cache_prefill.shape[4]
    head_dim = pair_width // 2
    members = lax.dynamic_slice_in_dim(req_order, req_index * group_size, group_size)
    member_stretch = jnp.take(stretch_lens, members)
    member_prefix = jnp.take(prefix_lens, members)
    ordered_prefix = jnp.take(prefix_lens, req_order)
    positions = head_index * prefix_rows + jnp.arange(prefix_rows, dtype=jnp.int32)
    keep = positions[None, :] < ordered_prefix[:, None]
    local_layers = cache_prefill.shape[0]
    slots = cache_prefill.shape[1]
    heads = cache_prefill.shape[3]
    devices = req_count * head_count
    chunks = []
    deferred = []
    for layer in range(local_layers):
        dealt_cache = jnp.where(
            keep[:, :, None, None],
            jnp.take(cache_prefill[layer], req_order, axis=0),
            jnp.zeros((), cache_prefill.dtype),
        )
        outgoing = (
            dealt_cache.reshape(req_count, group_size, prefix_rows, head_count, heads // head_count, pair_width)
            .transpose(0, 3, 1, 2, 4, 5)
            .reshape(devices, group_size, prefix_rows, heads // head_count, pair_width)
        )
        if layer == 0:
            chunks.append(land(lax.all_to_all(outgoing, ("req", "head"), 0, 0, tiled=True), req_count, head_count))
        else:
            deferred.append(outgoing)
    current = chunks[0][0]
    dealt_acts = jnp.take(stretch_acts, req_order, axis=0)
    dealt_rows = lax.all_to_all(dealt_acts, "req", split_axis=0, concat_axis=1, tiled=True).reshape(
        group_size, req_count, stretch_rows, features
    )
    gathered = lax.all_gather(dealt_rows, "head", axis=2, tiled=True)
    normed = (
        layer_norm(gathered.astype(jnp.float32), attn_gain)
        .astype(jnp.bfloat16)
        .reshape(group_size * stretch_max, features)
    )
    mixed = jnp.dot(
        normed,
        in_weight.reshape(features, heads_here * 3 * head_dim),
        preferred_element_type=jnp.float32,
    )
    mixed = mixed.reshape(group_size, stretch_max, heads_here, 3 * head_dim).astype(jnp.bfloat16)
    contexts = []
    for member in range(group_size):
        pairs = jnp.concatenate([current[member], mixed[member, :, :, head_dim:]], axis=0)
        contexts.append(
            attend(mixed[member, :, :, :head_dim], pairs, member_prefix[member], slopes, head_dim)
        )
    context = jnp.concatenate(contexts, axis=0)
    partial_attn = jnp.dot(
        context,
        out_weight.reshape(heads_here * head_dim, features),
        preferred_element_type=jnp.float32,
    )
    partial_attn = partial_attn.reshape(group_size, req_count, span_rows, features)
    attn_rows = head_sum(partial_attn, head_count, stretch_rows)
    residual_rows = dealt_rows.astype(jnp.float32) + attn_rows
    normed_rows = layer_norm(residual_rows, mlp_gain).astype(jnp.bfloat16)
    normed_all = lax.all_gather(normed_rows, "head", axis=2, tiled=True)
    deferred, normed_all = lax.optimization_barrier((deferred, normed_all))
    for outgoing in deferred:
        chunks.append(land(lax.all_to_all(outgoing, ("req", "head"), 0, 0, tiled=True), req_count, head_count))
    relaid = jnp.stack(chunks, axis=1).reshape((req_count * local_layers,) + chunks[0].shape[1:])
    inner = jax.nn.gelu(
        jnp.dot(
            normed_all.reshape(group_size * stretch_max, features),
            up_weight,
            preferred_element_type=jnp.float32,
        ),
        approximate=False,
    ).astype(jnp.bfloat16)
    partial_mlp = jnp.dot(inner, down_weight, preferred_element_type=jnp.float32).reshape(
        group_size, req_count, span_rows, features
    )
    mlp_rows = head_sum(partial_mlp, head_count, stretch_rows)
    relaid, mlp_rows = lax.optimization_barrier((relaid, mlp_rows))
    row_number = (
        jnp.arange(req_count, dtype=jnp.int32)[:, None] * head_count + head_index
    ) * stretch_rows + jnp.arange(stretch_rows, dtype=jnp.int32)[None, :]
    usable = row_number[None] < member_stretch[:, None, None]
    result = jnp.where(
        usable[..., None], residual_rows + mlp_rows, jnp.zeros((), jnp.float32)
    ).astype(jnp.bfloat16)
    returned = lax.all_to_all(result, "req", split_axis=1, concat_axis=0, tiled=True).reshape(
        requests, stretch_rows, features
    )
    inverse = jnp.argsort(req_order)
    layer_out = jnp.take(returned, inverse, axis=0)
    return (layer_out, relaid)


def solution(mesh):
    return jax.shard_map(
        local,
        mesh=mesh,
        in_specs=(
            P(None, ("req", "head"), None),
            P("req", None, "head", None, None),
            P(),
            P(),
            P(),
            P(),
            P(None, "head", None),
            P("head"),
            P("head", None, None),
            P(),
            P(None, "head"),
            P("head", None),
        ),
        out_specs=(P(None, ("req", "head"), None), P(None, "req", None, "head", None)),
        check_vma=False,
    )
```

```python
import math

import jax
import jax.numpy as jnp
from jax import lax
from jax.sharding import PartitionSpec as P

EPSILON = 1e-05


def layer_norm(values, gain):
    average = jnp.mean(values, axis=-1, keepdims=True)
    centred = values - average
    variance = jnp.mean(centred * centred, axis=-1, keepdims=True)
    return centred * lax.rsqrt(variance + EPSILON) * gain.astype(jnp.float32)


def attend(queries, pairs, prefix_len, slopes, head_dim):
    stretch = queries.shape[0]
    prefix = pairs.shape[0] - stretch
    keys_part = pairs[..., :head_dim]
    values_part = pairs[..., head_dim:]
    scores = jnp.einsum("qhd,khd->hqk", queries, keys_part, preferred_element_type=jnp.float32) * (
        1.0 / math.sqrt(head_dim)
    )
    row_index = jnp.arange(stretch, dtype=jnp.int32)
    key_index = jnp.arange(prefix + stretch, dtype=jnp.int32)
    in_prefix = key_index < prefix
    query_pos = prefix_len + row_index
    key_pos = jnp.where(in_prefix, key_index, prefix_len + key_index - prefix)
    allowed = jnp.where(
        in_prefix[None, :],
        key_index[None, :] < prefix_len,
        (key_index - prefix)[None, :] <= row_index[:, None],
    )
    distance = (query_pos[:, None] - key_pos[None, :]).astype(jnp.float32)
    scores = scores - slopes[:, None, None] * distance[None]
    scores = jnp.where(allowed[None], scores, -jnp.inf)
    highest = jnp.max(scores, axis=-1, keepdims=True)
    expo = jnp.exp(scores - highest)
    soft = (expo / jnp.sum(expo, axis=-1, keepdims=True)).astype(jnp.bfloat16)
    context = jnp.einsum("hqk,khd->qhd", soft, values_part, preferred_element_type=jnp.float32)
    return context.astype(jnp.bfloat16).reshape(stretch, -1)


def head_sum(partial, head_count, stretch_rows):
    inner_size = 4 if head_count % 4 == 0 else head_count
    outer_size = head_count // inner_size
    me = lax.axis_index("head")
    outer_me, inner_me = me // inner_size, me % inner_size
    blocks = partial.astype(jnp.bfloat16).reshape(
        partial.shape[:2] + (outer_size, inner_size, stretch_rows) + partial.shape[3:]
    )
    level_one = lax.dynamic_index_in_dim(blocks, inner_me, 3, False).astype(jnp.float32)
    for shift in range(1, inner_size):
        pairs = [(j, (j // inner_size) * inner_size + (j % inner_size + shift) % inner_size) for j in range(head_count)]
        sent = lax.dynamic_index_in_dim(blocks, (inner_me + shift) % inner_size, 3, False)
        level_one = level_one + lax.ppermute(sent, "head", pairs).astype(jnp.float32)
    rounded_one = level_one.astype(jnp.bfloat16)
    total = lax.dynamic_index_in_dim(level_one, outer_me, 2, False)
    for shift in range(1, outer_size):
        pairs = [(j, ((j // inner_size + shift) % outer_size) * inner_size + j % inner_size) for j in range(head_count)]
        sent = lax.dynamic_index_in_dim(rounded_one, (outer_me + shift) % outer_size, 2, False)
        total = total + lax.ppermute(sent, "head", pairs).astype(jnp.float32)
    return total


def land(incoming, req_count, head_count):
    shape = (req_count, head_count) + incoming.shape[1:]
    landed = incoming.reshape(shape).transpose(0, 2, 1, 3, 4, 5)
    return landed.reshape(landed.shape[:2] + (-1,) + landed.shape[4:])


def local(
    stretch_acts,
    cache_prefill,
    stretch_lens,
    prefix_lens,
    req_order,
    attn_gain,
    in_weight,
    slopes,
    out_weight,
    mlp_gain,
    up_weight,
    down_weight,
):
    req_count = lax.axis_size("req")
    head_count = lax.axis_size("head")
    req_index = lax.axis_index("req")
    head_index = lax.axis_index("head")
    requests = stretch_acts.shape[0]
    stretch_rows = stretch_acts.shape[1]
    features = stretch_acts.shape[2]
    group_size = requests // req_count
    span_rows = head_count * stretch_rows
    stretch_max = req_count * span_rows
    prefix_rows = cache_prefill.shape[2]
    heads_here = in_weight.shape[1]
    pair_width = cache_prefill.shape[4]
    head_dim = pair_width // 2
    members = lax.dynamic_slice_in_dim(req_order, req_index * group_size, group_size)
    member_stretch = jnp.take(stretch_lens, members)
    member_prefix = jnp.take(prefix_lens, members)
    ordered_prefix = jnp.take(prefix_lens, req_order)
    positions = head_index * prefix_rows + jnp.arange(prefix_rows, dtype=jnp.int32)
    keep = positions[None, :] < ordered_prefix[:, None]
    local_layers = cache_prefill.shape[0]
    slots = cache_prefill.shape[1]
    heads = cache_prefill.shape[3]
    devices = req_count * head_count
    chunks = []
    deferred = []
    later_layers = cache_prefill[1:]
    for layer in range(local_layers):
        source = cache_prefill[0] if layer == 0 else later_layers[layer - 1]
        dealt_cache = jnp.where(
            keep[:, :, None, None],
            jnp.take(source, req_order, axis=0),
            jnp.zeros((), cache_prefill.dtype),
        )
        outgoing = (
            dealt_cache.reshape(req_count, group_size, prefix_rows, head_count, heads // head_count, pair_width)
            .transpose(0, 3, 1, 2, 4, 5)
            .reshape(devices, group_size, prefix_rows, heads // head_count, pair_width)
        )
        if layer == 0:
            incoming = lax.all_to_all(outgoing, ("req", "head"), 0, 0, tiled=True)
            incoming, later_layers = lax.optimization_barrier((incoming, later_layers))
            chunks.append(land(incoming, req_count, head_count))
        else:
            deferred.append(outgoing)
    current = chunks[0][0]
    dealt_acts = jnp.take(stretch_acts, req_order, axis=0)
    dealt_rows = lax.all_to_all(dealt_acts, "req", split_axis=0, concat_axis=1, tiled=True).reshape(
        group_size, req_count, stretch_rows, features
    )
    gathered = lax.all_gather(dealt_rows, "head", axis=2, tiled=True)
    normed = (
        layer_norm(gathered.astype(jnp.float32), attn_gain)
        .astype(jnp.bfloat16)
        .reshape(group_size * stretch_max, features)
    )
    mixed = jnp.dot(
        normed,
        in_weight.reshape(features, heads_here * 3 * head_dim),
        preferred_element_type=jnp.float32,
    )
    mixed = mixed.reshape(group_size, stretch_max, heads_here, 3 * head_dim).astype(jnp.bfloat16)
    contexts = []
    for member in range(group_size):
        pairs = jnp.concatenate([current[member], mixed[member, :, :, head_dim:]], axis=0)
        contexts.append(
            attend(mixed[member, :, :, :head_dim], pairs, member_prefix[member], slopes, head_dim)
        )
    context = jnp.concatenate(contexts, axis=0)
    partial_attn = jnp.dot(
        context,
        out_weight.reshape(heads_here * head_dim, features),
        preferred_element_type=jnp.float32,
    )
    partial_attn = partial_attn.reshape(group_size, req_count, span_rows, features)
    attn_rows = head_sum(partial_attn, head_count, stretch_rows)
    residual_rows = dealt_rows.astype(jnp.float32) + attn_rows
    normed_rows = layer_norm(residual_rows, mlp_gain).astype(jnp.bfloat16)
    normed_all = lax.all_gather(normed_rows, "head", axis=2, tiled=True)
    deferred, normed_all = lax.optimization_barrier((deferred, normed_all))
    for outgoing in deferred:
        chunks.append(land(lax.all_to_all(outgoing, ("req", "head"), 0, 0, tiled=True), req_count, head_count))
    relaid = jnp.stack(chunks, axis=1).reshape((req_count * local_layers,) + chunks[0].shape[1:])
    inner = jax.nn.gelu(
        jnp.dot(
            normed_all.reshape(group_size * stretch_max, features),
            up_weight,
            preferred_element_type=jnp.float32,
        ),
        approximate=False,
    ).astype(jnp.bfloat16)
    partial_mlp = jnp.dot(inner, down_weight, preferred_element_type=jnp.float32).reshape(
        group_size, req_count, span_rows, features
    )
    mlp_rows = head_sum(partial_mlp, head_count, stretch_rows)
    relaid, mlp_rows = lax.optimization_barrier((relaid, mlp_rows))
    row_number = (
        jnp.arange(req_count, dtype=jnp.int32)[:, None] * head_count + head_index
    ) * stretch_rows + jnp.arange(stretch_rows, dtype=jnp.int32)[None, :]
    usable = row_number[None] < member_stretch[:, None, None]
    result = jnp.where(
        usable[..., None], residual_rows + mlp_rows, jnp.zeros((), jnp.float32)
    ).astype(jnp.bfloat16)
    returned = lax.all_to_all(result, "req", split_axis=1, concat_axis=0, tiled=True).reshape(
        requests, stretch_rows, features
    )
    inverse = jnp.argsort(req_order)
    layer_out = jnp.take(returned, inverse, axis=0)
    return (layer_out, relaid)


def solution(mesh):
    return jax.shard_map(
        local,
        mesh=mesh,
        in_specs=(
            P(None, ("req", "head"), None),
            P("req", None, "head", None, None),
            P(),
            P(),
            P(),
            P(),
            P(None, "head", None),
            P("head"),
            P("head", None, None),
            P(),
            P(None, "head"),
            P("head", None),
        ),
        out_specs=(P(None, ("req", "head"), None), P(None, "req", None, "head", None)),
        check_vma=False,
    )
```

```python
import math

import jax
import jax.numpy as jnp
from jax import lax
from jax.sharding import PartitionSpec as P

EPSILON = 1e-05


def layer_norm(values, gain):
    average = jnp.mean(values, axis=-1, keepdims=True)
    centred = values - average
    variance = jnp.mean(centred * centred, axis=-1, keepdims=True)
    return centred * lax.rsqrt(variance + EPSILON) * gain.astype(jnp.float32)


def attend(queries, pairs, prefix_len, slopes, head_dim):
    stretch = queries.shape[0]
    prefix = pairs.shape[0] - stretch
    keys_part = pairs[..., :head_dim]
    values_part = pairs[..., head_dim:]
    scores = jnp.einsum("qhd,khd->hqk", queries, keys_part, preferred_element_type=jnp.float32) * (
        1.0 / math.sqrt(head_dim)
    )
    row_index = jnp.arange(stretch, dtype=jnp.int32)
    key_index = jnp.arange(prefix + stretch, dtype=jnp.int32)
    in_prefix = key_index < prefix
    query_pos = prefix_len + row_index
    key_pos = jnp.where(in_prefix, key_index, prefix_len + key_index - prefix)
    allowed = jnp.where(
        in_prefix[None, :],
        key_index[None, :] < prefix_len,
        (key_index - prefix)[None, :] <= row_index[:, None],
    )
    distance = (query_pos[:, None] - key_pos[None, :]).astype(jnp.float32)
    scores = scores - slopes[:, None, None] * distance[None]
    scores = jnp.where(allowed[None], scores, -jnp.inf)
    highest = jnp.max(scores, axis=-1, keepdims=True)
    expo = jnp.exp(scores - highest)
    soft = (expo / jnp.sum(expo, axis=-1, keepdims=True)).astype(jnp.bfloat16)
    context = jnp.einsum("hqk,khd->qhd", soft, values_part, preferred_element_type=jnp.float32)
    return context.astype(jnp.bfloat16).reshape(stretch, -1)


def head_sum(partial, head_count, stretch_rows):
    inner_size = 4 if head_count % 4 == 0 else head_count
    outer_size = head_count // inner_size
    me = lax.axis_index("head")
    outer_me, inner_me = me // inner_size, me % inner_size
    blocks = partial.astype(jnp.bfloat16).reshape(
        partial.shape[:2] + (outer_size, inner_size, stretch_rows) + partial.shape[3:]
    )
    level_one = lax.dynamic_index_in_dim(blocks, inner_me, 3, False).astype(jnp.float32)
    for shift in range(1, inner_size):
        pairs = [(j, (j // inner_size) * inner_size + (j % inner_size + shift) % inner_size) for j in range(head_count)]
        sent = lax.dynamic_index_in_dim(blocks, (inner_me + shift) % inner_size, 3, False)
        level_one = level_one + lax.ppermute(sent, "head", pairs).astype(jnp.float32)
    rounded_one = level_one.astype(jnp.bfloat16)
    total = lax.dynamic_index_in_dim(level_one, outer_me, 2, False)
    for shift in range(1, outer_size):
        pairs = [(j, ((j // inner_size + shift) % outer_size) * inner_size + j % inner_size) for j in range(head_count)]
        sent = lax.dynamic_index_in_dim(rounded_one, (outer_me + shift) % outer_size, 2, False)
        total = total + lax.ppermute(sent, "head", pairs).astype(jnp.float32)
    return total


def land(incoming, req_count, head_count):
    shape = (req_count, head_count) + incoming.shape[1:]
    landed = incoming.reshape(shape).transpose(0, 2, 1, 3, 4, 5)
    return landed.reshape(landed.shape[:2] + (-1,) + landed.shape[4:])


def local(
    stretch_acts,
    cache_prefill,
    stretch_lens,
    prefix_lens,
    req_order,
    attn_gain,
    in_weight,
    slopes,
    out_weight,
    mlp_gain,
    up_weight,
    down_weight,
):
    req_count = lax.axis_size("req")
    head_count = lax.axis_size("head")
    req_index = lax.axis_index("req")
    head_index = lax.axis_index("head")
    requests = stretch_acts.shape[0]
    stretch_rows = stretch_acts.shape[1]
    features = stretch_acts.shape[2]
    group_size = requests // req_count
    span_rows = head_count * stretch_rows
    stretch_max = req_count * span_rows
    prefix_rows = cache_prefill.shape[2]
    heads_here = in_weight.shape[1]
    pair_width = cache_prefill.shape[4]
    head_dim = pair_width // 2
    members = lax.dynamic_slice_in_dim(req_order, req_index * group_size, group_size)
    member_stretch = jnp.take(stretch_lens, members)
    member_prefix = jnp.take(prefix_lens, members)
    ordered_prefix = jnp.take(prefix_lens, req_order)
    positions = head_index * prefix_rows + jnp.arange(prefix_rows, dtype=jnp.int32)
    keep = positions[None, :] < ordered_prefix[:, None]
    local_layers = cache_prefill.shape[0]
    slots = cache_prefill.shape[1]
    heads = cache_prefill.shape[3]
    devices = req_count * head_count
    chunks = []
    deferred = []
    later_layers = cache_prefill[1:]
    for layer in range(local_layers):
        source = cache_prefill[0] if layer == 0 else later_layers[layer - 1]
        dealt_cache = jnp.where(
            keep[:, :, None, None],
            jnp.take(source, req_order, axis=0),
            jnp.zeros((), cache_prefill.dtype),
        )
        outgoing = (
            dealt_cache.reshape(req_count, group_size, prefix_rows, head_count, heads // head_count, pair_width)
            .transpose(0, 3, 1, 2, 4, 5)
            .reshape(devices, group_size, prefix_rows, heads // head_count, pair_width)
        )
        if layer == 0:
            incoming = lax.all_to_all(outgoing, ("req", "head"), 0, 0, tiled=True)
            incoming, later_layers = lax.optimization_barrier((incoming, later_layers))
            chunks.append(land(incoming, req_count, head_count))
        else:
            deferred.append(outgoing)
    current = chunks[0][0]
    for outgoing in deferred:
        chunks.append(land(lax.all_to_all(outgoing, ("req", "head"), 0, 0, tiled=True), req_count, head_count))
    dealt_acts = jnp.take(stretch_acts, req_order, axis=0)
    dealt_rows = lax.all_to_all(dealt_acts, "req", split_axis=0, concat_axis=1, tiled=True).reshape(
        group_size, req_count, stretch_rows, features
    )
    gathered = lax.all_gather(dealt_rows, "head", axis=2, tiled=True)
    normed = (
        layer_norm(gathered.astype(jnp.float32), attn_gain)
        .astype(jnp.bfloat16)
        .reshape(group_size * stretch_max, features)
    )
    mixed = jnp.dot(
        normed,
        in_weight.reshape(features, heads_here * 3 * head_dim),
        preferred_element_type=jnp.float32,
    )
    mixed = mixed.reshape(group_size, stretch_max, heads_here, 3 * head_dim).astype(jnp.bfloat16)
    contexts = []
    for member in range(group_size):
        pairs = jnp.concatenate([current[member], mixed[member, :, :, head_dim:]], axis=0)
        contexts.append(
            attend(mixed[member, :, :, :head_dim], pairs, member_prefix[member], slopes, head_dim)
        )
    context = jnp.concatenate(contexts, axis=0)
    partial_attn = jnp.dot(
        context,
        out_weight.reshape(heads_here * head_dim, features),
        preferred_element_type=jnp.float32,
    )
    partial_attn = partial_attn.reshape(group_size, req_count, span_rows, features)
    attn_rows = head_sum(partial_attn, head_count, stretch_rows)
    attn_rows, later_chunks = lax.optimization_barrier((attn_rows, chunks[1:]))
    relaid = jnp.stack(chunks[:1] + later_chunks, axis=1).reshape((req_count * local_layers,) + chunks[0].shape[1:])
    residual_rows = dealt_rows.astype(jnp.float32) + attn_rows
    normed_rows = layer_norm(residual_rows, mlp_gain).astype(jnp.bfloat16)
    normed_all = lax.all_gather(normed_rows, "head", axis=2, tiled=True)
    inner = jax.nn.gelu(
        jnp.dot(
            normed_all.reshape(group_size * stretch_max, features),
            up_weight,
            preferred_element_type=jnp.float32,
        ),
        approximate=False,
    ).astype(jnp.bfloat16)
    partial_mlp = jnp.dot(inner, down_weight, preferred_element_type=jnp.float32).reshape(
        group_size, req_count, span_rows, features
    )
    mlp_rows = head_sum(partial_mlp, head_count, stretch_rows)
    relaid, mlp_rows = lax.optimization_barrier((relaid, mlp_rows))
    row_number = (
        jnp.arange(req_count, dtype=jnp.int32)[:, None] * head_count + head_index
    ) * stretch_rows + jnp.arange(stretch_rows, dtype=jnp.int32)[None, :]
    usable = row_number[None] < member_stretch[:, None, None]
    result = jnp.where(
        usable[..., None], residual_rows + mlp_rows, jnp.zeros((), jnp.float32)
    ).astype(jnp.bfloat16)
    returned = lax.all_to_all(result, "req", split_axis=1, concat_axis=0, tiled=True).reshape(
        requests, stretch_rows, features
    )
    inverse = jnp.argsort(req_order)
    layer_out = jnp.take(returned, inverse, axis=0)
    return (layer_out, relaid)


def solution(mesh):
    return jax.shard_map(
        local,
        mesh=mesh,
        in_specs=(
            P(None, ("req", "head"), None),
            P("req", None, "head", None, None),
            P(),
            P(),
            P(),
            P(),
            P(None, "head", None),
            P("head"),
            P("head", None, None),
            P(),
            P(None, "head"),
            P("head", None),
        ),
        out_specs=(P(None, ("req", "head"), None), P(None, "req", None, "head", None)),
        check_vma=False,
    )
```

```python
import math

import jax
import jax.numpy as jnp
from jax import lax
from jax.sharding import PartitionSpec as P

EPSILON = 1e-05


def layer_norm(values, gain):
    average = jnp.mean(values, axis=-1, keepdims=True)
    centred = values - average
    variance = jnp.mean(centred * centred, axis=-1, keepdims=True)
    return centred * lax.rsqrt(variance + EPSILON) * gain.astype(jnp.float32)


def attend(queries, pairs, prefix_len, slopes, head_dim):
    stretch = queries.shape[0]
    prefix = pairs.shape[0] - stretch
    keys_part = pairs[..., :head_dim]
    values_part = pairs[..., head_dim:]
    scores = jnp.einsum("qhd,khd->hqk", queries, keys_part, preferred_element_type=jnp.float32) * (
        1.0 / math.sqrt(head_dim)
    )
    row_index = jnp.arange(stretch, dtype=jnp.int32)
    key_index = jnp.arange(prefix + stretch, dtype=jnp.int32)
    in_prefix = key_index < prefix
    query_pos = prefix_len + row_index
    key_pos = jnp.where(in_prefix, key_index, prefix_len + key_index - prefix)
    allowed = jnp.where(
        in_prefix[None, :],
        key_index[None, :] < prefix_len,
        (key_index - prefix)[None, :] <= row_index[:, None],
    )
    distance = (query_pos[:, None] - key_pos[None, :]).astype(jnp.float32)
    scores = scores - slopes[:, None, None] * distance[None]
    scores = jnp.where(allowed[None], scores, -jnp.inf)
    highest = jnp.max(scores, axis=-1, keepdims=True)
    expo = jnp.exp(scores - highest)
    soft = (expo / jnp.sum(expo, axis=-1, keepdims=True)).astype(jnp.bfloat16)
    context = jnp.einsum("hqk,khd->qhd", soft, values_part, preferred_element_type=jnp.float32)
    return context.astype(jnp.bfloat16).reshape(stretch, -1)


def head_sum(partial, head_count, stretch_rows):
    inner_size = 4 if head_count % 4 == 0 else head_count
    outer_size = head_count // inner_size
    me = lax.axis_index("head")
    outer_me, inner_me = me // inner_size, me % inner_size
    blocks = partial.astype(jnp.bfloat16).reshape(
        partial.shape[:2] + (outer_size, inner_size, stretch_rows) + partial.shape[3:]
    )
    level_one = lax.dynamic_index_in_dim(blocks, inner_me, 3, False).astype(jnp.float32)
    for shift in range(1, inner_size):
        pairs = [(j, (j // inner_size) * inner_size + (j % inner_size + shift) % inner_size) for j in range(head_count)]
        sent = lax.dynamic_index_in_dim(blocks, (inner_me + shift) % inner_size, 3, False)
        level_one = level_one + lax.ppermute(sent, "head", pairs).astype(jnp.float32)
    rounded_one = level_one.astype(jnp.bfloat16)
    total = lax.dynamic_index_in_dim(level_one, outer_me, 2, False)
    for shift in range(1, outer_size):
        pairs = [(j, ((j // inner_size + shift) % outer_size) * inner_size + j % inner_size) for j in range(head_count)]
        sent = lax.dynamic_index_in_dim(rounded_one, (outer_me + shift) % outer_size, 2, False)
        total = total + lax.ppermute(sent, "head", pairs).astype(jnp.float32)
    return total


def head_gather(rows, head_count):
    inner_size = 4 if head_count % 4 == 0 else head_count
    outer_size = head_count // inner_size
    me = lax.axis_index("head")
    outer_me, inner_me = me // inner_size, me % inner_size
    held = [rows]
    for shift in range(1, outer_size):
        pairs = [(j, ((j // inner_size + shift) % outer_size) * inner_size + j % inner_size) for j in range(head_count)]
        held.append(lax.ppermute(rows, "head", pairs))
    by_outer = jnp.take(jnp.stack(held), (outer_me - jnp.arange(outer_size)) % outer_size, axis=0)
    held = [by_outer]
    for shift in range(1, inner_size):
        pairs = [(j, (j // inner_size) * inner_size + (j % inner_size + shift) % inner_size) for j in range(head_count)]
        held.append(lax.ppermute(by_outer, "head", pairs))
    by_inner = jnp.take(jnp.stack(held), (inner_me - jnp.arange(inner_size)) % inner_size, axis=0)
    gathered = jnp.moveaxis(by_inner, (0, 1), (3, 2))
    return gathered.reshape(rows.shape[:2] + (head_count * rows.shape[2],) + rows.shape[3:])


def land(incoming, req_count, head_count):
    shape = (req_count, head_count) + incoming.shape[1:]
    landed = incoming.reshape(shape).transpose(0, 2, 1, 3, 4, 5)
    return landed.reshape(landed.shape[:2] + (-1,) + landed.shape[4:])


def local(
    stretch_acts,
    cache_prefill,
    stretch_lens,
    prefix_lens,
    req_order,
    attn_gain,
    in_weight,
    slopes,
    out_weight,
    mlp_gain,
    up_weight,
    down_weight,
):
    req_count = lax.axis_size("req")
    head_count = lax.axis_size("head")
    req_index = lax.axis_index("req")
    head_index = lax.axis_index("head")
    requests = stretch_acts.shape[0]
    stretch_rows = stretch_acts.shape[1]
    features = stretch_acts.shape[2]
    group_size = requests // req_count
    span_rows = head_count * stretch_rows
    stretch_max = req_count * span_rows
    prefix_rows = cache_prefill.shape[2]
    heads_here = in_weight.shape[1]
    pair_width = cache_prefill.shape[4]
    head_dim = pair_width // 2
    members = lax.dynamic_slice_in_dim(req_order, req_index * group_size, group_size)
    member_stretch = jnp.take(stretch_lens, members)
    member_prefix = jnp.take(prefix_lens, members)
    ordered_prefix = jnp.take(prefix_lens, req_order)
    positions = head_index * prefix_rows + jnp.arange(prefix_rows, dtype=jnp.int32)
    keep = positions[None, :] < ordered_prefix[:, None]
    local_layers = cache_prefill.shape[0]
    slots = cache_prefill.shape[1]
    heads = cache_prefill.shape[3]
    devices = req_count * head_count
    dealt_acts = jnp.take(stretch_acts, req_order, axis=0)
    dealt_rows = lax.all_to_all(dealt_acts, "req", split_axis=0, concat_axis=1, tiled=True).reshape(
        group_size, req_count, stretch_rows, features
    )
    gathered = head_gather(dealt_rows, head_count)
    chunks = []
    deferred = []
    later_layers = cache_prefill[1:]
    for layer in range(local_layers):
        source = cache_prefill[0] if layer == 0 else later_layers[layer - 1]
        dealt_cache = jnp.where(
            keep[:, :, None, None],
            jnp.take(source, req_order, axis=0),
            jnp.zeros((), cache_prefill.dtype),
        )
        outgoing = (
            dealt_cache.reshape(req_count, group_size, prefix_rows, head_count, heads // head_count, pair_width)
            .transpose(0, 3, 1, 2, 4, 5)
            .reshape(devices, group_size, prefix_rows, heads // head_count, pair_width)
        )
        if layer == 0:
            outgoing, gathered = lax.optimization_barrier((outgoing, gathered))
            incoming = lax.all_to_all(outgoing, ("req", "head"), 0, 0, tiled=True)
            incoming, later_layers = lax.optimization_barrier((incoming, later_layers))
            chunks.append(land(incoming, req_count, head_count))
        else:
            deferred.append(outgoing)
    current = chunks[0][0]
    normed = (
        layer_norm(gathered.astype(jnp.float32), attn_gain)
        .astype(jnp.bfloat16)
        .reshape(group_size * stretch_max, features)
    )
    mixed = jnp.dot(
        normed,
        in_weight.reshape(features, heads_here * 3 * head_dim),
        preferred_element_type=jnp.float32,
    )
    mixed = mixed.reshape(group_size, stretch_max, heads_here, 3 * head_dim).astype(jnp.bfloat16)
    contexts = []
    for member in range(group_size):
        pairs = jnp.concatenate([current[member], mixed[member, :, :, head_dim:]], axis=0)
        contexts.append(
            attend(mixed[member, :, :, :head_dim], pairs, member_prefix[member], slopes, head_dim)
        )
    context = jnp.concatenate(contexts, axis=0)
    partial_attn = jnp.dot(
        context,
        out_weight.reshape(heads_here * head_dim, features),
        preferred_element_type=jnp.float32,
    )
    partial_attn = partial_attn.reshape(group_size, req_count, span_rows, features)
    attn_rows = head_sum(partial_attn, head_count, stretch_rows)
    residual_rows = dealt_rows.astype(jnp.float32) + attn_rows
    normed_rows = layer_norm(residual_rows, mlp_gain).astype(jnp.bfloat16)
    normed_all = head_gather(normed_rows, head_count)
    deferred, normed_all = lax.optimization_barrier((deferred, normed_all))
    for outgoing in deferred:
        chunks.append(land(lax.all_to_all(outgoing, ("req", "head"), 0, 0, tiled=True), req_count, head_count))
    relaid = jnp.stack(chunks, axis=1).reshape((req_count * local_layers,) + chunks[0].shape[1:])
    inner = jax.nn.gelu(
        jnp.dot(
            normed_all.reshape(group_size * stretch_max, features),
            up_weight,
            preferred_element_type=jnp.float32,
        ),
        approximate=False,
    ).astype(jnp.bfloat16)
    partial_mlp = jnp.dot(inner, down_weight, preferred_element_type=jnp.float32).reshape(
        group_size, req_count, span_rows, features
    )
    mlp_rows = head_sum(partial_mlp, head_count, stretch_rows)
    relaid, mlp_rows = lax.optimization_barrier((relaid, mlp_rows))
    row_number = (
        jnp.arange(req_count, dtype=jnp.int32)[:, None] * head_count + head_index
    ) * stretch_rows + jnp.arange(stretch_rows, dtype=jnp.int32)[None, :]
    usable = row_number[None] < member_stretch[:, None, None]
    result = jnp.where(
        usable[..., None], residual_rows + mlp_rows, jnp.zeros((), jnp.float32)
    ).astype(jnp.bfloat16)
    returned = lax.all_to_all(result, "req", split_axis=1, concat_axis=0, tiled=True).reshape(
        requests, stretch_rows, features
    )
    inverse = jnp.argsort(req_order)
    layer_out = jnp.take(returned, inverse, axis=0)
    return (layer_out, relaid)


def solution(mesh):
    return jax.shard_map(
        local,
        mesh=mesh,
        in_specs=(
            P(None, ("req", "head"), None),
            P("req", None, "head", None, None),
            P(),
            P(),
            P(),
            P(),
            P(None, "head", None),
            P("head"),
            P("head", None, None),
            P(),
            P(None, "head"),
            P("head", None),
        ),
        out_specs=(P(None, ("req", "head"), None), P(None, "req", None, "head", None)),
        check_vma=False,
    )
```

```python
import math

import jax
import jax.numpy as jnp
from jax import lax
from jax.sharding import PartitionSpec as P

EPSILON = 1e-05


def layer_norm(values, gain):
    average = jnp.mean(values, axis=-1, keepdims=True)
    centred = values - average
    variance = jnp.mean(centred * centred, axis=-1, keepdims=True)
    return centred * lax.rsqrt(variance + EPSILON) * gain.astype(jnp.float32)


def attend(queries, pairs, prefix_len, slopes, head_dim):
    stretch = queries.shape[0]
    prefix = pairs.shape[0] - stretch
    keys_part = pairs[..., :head_dim]
    values_part = pairs[..., head_dim:]
    scores = jnp.einsum("qhd,khd->hqk", queries, keys_part, preferred_element_type=jnp.float32) * (
        1.0 / math.sqrt(head_dim)
    )
    row_index = jnp.arange(stretch, dtype=jnp.int32)
    key_index = jnp.arange(prefix + stretch, dtype=jnp.int32)
    in_prefix = key_index < prefix
    query_pos = prefix_len + row_index
    key_pos = jnp.where(in_prefix, key_index, prefix_len + key_index - prefix)
    allowed = jnp.where(
        in_prefix[None, :],
        key_index[None, :] < prefix_len,
        (key_index - prefix)[None, :] <= row_index[:, None],
    )
    distance = (query_pos[:, None] - key_pos[None, :]).astype(jnp.float32)
    scores = scores - slopes[:, None, None] * distance[None]
    scores = jnp.where(allowed[None], scores, -jnp.inf)
    highest = jnp.max(scores, axis=-1, keepdims=True)
    expo = jnp.exp(scores - highest)
    soft = (expo / jnp.sum(expo, axis=-1, keepdims=True)).astype(jnp.bfloat16)
    context = jnp.einsum("hqk,khd->qhd", soft, values_part, preferred_element_type=jnp.float32)
    return context.astype(jnp.bfloat16).reshape(stretch, -1)


def head_sum(partial, head_count, stretch_rows):
    inner_size = 4 if head_count % 4 == 0 else head_count
    outer_size = head_count // inner_size
    me = lax.axis_index("head")
    outer_me, inner_me = me // inner_size, me % inner_size
    blocks = partial.astype(jnp.bfloat16).reshape(
        partial.shape[:2] + (outer_size, inner_size, stretch_rows) + partial.shape[3:]
    )
    level_one = lax.dynamic_index_in_dim(blocks, inner_me, 3, False).astype(jnp.float32)
    for shift in range(1, inner_size):
        pairs = [(j, (j // inner_size) * inner_size + (j % inner_size + shift) % inner_size) for j in range(head_count)]
        sent = lax.dynamic_index_in_dim(blocks, (inner_me + shift) % inner_size, 3, False)
        level_one = level_one + lax.ppermute(sent, "head", pairs).astype(jnp.float32)
    rounded_one = level_one.astype(jnp.bfloat16)
    total = lax.dynamic_index_in_dim(level_one, outer_me, 2, False)
    for shift in range(1, outer_size):
        pairs = [(j, ((j // inner_size + shift) % outer_size) * inner_size + j % inner_size) for j in range(head_count)]
        sent = lax.dynamic_index_in_dim(rounded_one, (outer_me + shift) % outer_size, 2, False)
        total = total + lax.ppermute(sent, "head", pairs).astype(jnp.float32)
    return total


def head_gather(rows, head_count):
    inner_size = 4 if head_count % 4 == 0 else head_count
    outer_size = head_count // inner_size
    me = lax.axis_index("head")
    outer_me, inner_me = me // inner_size, me % inner_size
    held = [rows]
    for shift in range(1, outer_size):
        pairs = [(j, ((j // inner_size + shift) % outer_size) * inner_size + j % inner_size) for j in range(head_count)]
        held.append(lax.ppermute(rows, "head", pairs))
    by_outer = jnp.take(jnp.stack(held), (outer_me - jnp.arange(outer_size)) % outer_size, axis=0)
    held = [by_outer]
    for shift in range(1, inner_size):
        pairs = [(j, (j // inner_size) * inner_size + (j % inner_size + shift) % inner_size) for j in range(head_count)]
        held.append(lax.ppermute(by_outer, "head", pairs))
    by_inner = jnp.take(jnp.stack(held), (inner_me - jnp.arange(inner_size)) % inner_size, axis=0)
    gathered = jnp.moveaxis(by_inner, (0, 1), (3, 2))
    return gathered.reshape(rows.shape[:2] + (head_count * rows.shape[2],) + rows.shape[3:])


def land(incoming, req_count, head_count):
    shape = (req_count, head_count) + incoming.shape[1:]
    landed = incoming.reshape(shape).transpose(0, 2, 1, 3, 4, 5)
    return landed.reshape(landed.shape[:2] + (-1,) + landed.shape[4:])


def local(
    stretch_acts,
    cache_prefill,
    stretch_lens,
    prefix_lens,
    req_order,
    attn_gain,
    in_weight,
    slopes,
    out_weight,
    mlp_gain,
    up_weight,
    down_weight,
):
    req_count = lax.axis_size("req")
    head_count = lax.axis_size("head")
    req_index = lax.axis_index("req")
    head_index = lax.axis_index("head")
    requests = stretch_acts.shape[0]
    stretch_rows = stretch_acts.shape[1]
    features = stretch_acts.shape[2]
    group_size = requests // req_count
    span_rows = head_count * stretch_rows
    stretch_max = req_count * span_rows
    prefix_rows = cache_prefill.shape[2]
    heads_here = in_weight.shape[1]
    pair_width = cache_prefill.shape[4]
    head_dim = pair_width // 2
    members = lax.dynamic_slice_in_dim(req_order, req_index * group_size, group_size)
    member_stretch = jnp.take(stretch_lens, members)
    member_prefix = jnp.take(prefix_lens, members)
    ordered_prefix = jnp.take(prefix_lens, req_order)
    positions = head_index * prefix_rows + jnp.arange(prefix_rows, dtype=jnp.int32)
    keep = positions[None, :] < ordered_prefix[:, None]
    local_layers = cache_prefill.shape[0]
    slots = cache_prefill.shape[1]
    heads = cache_prefill.shape[3]
    devices = req_count * head_count
    chunks = []
    deferred = []
    later_layers = cache_prefill[1:]
    for layer in range(local_layers):
        source = cache_prefill[0] if layer == 0 else later_layers[layer - 1]
        dealt_cache = jnp.where(
            keep[:, :, None, None],
            jnp.take(source, req_order, axis=0),
            jnp.zeros((), cache_prefill.dtype),
        )
        outgoing = (
            dealt_cache.reshape(req_count, group_size, prefix_rows, head_count, heads // head_count, pair_width)
            .transpose(0, 3, 1, 2, 4, 5)
            .reshape(devices, group_size, prefix_rows, heads // head_count, pair_width)
        )
        if layer == 0:
            incoming = lax.all_to_all(outgoing, ("req", "head"), 0, 0, tiled=True)
            incoming, later_layers = lax.optimization_barrier((incoming, later_layers))
            chunks.append(land(incoming, req_count, head_count))
        else:
            deferred.append(outgoing)
    current = chunks[0][0]
    dealt_acts = jnp.take(stretch_acts, req_order, axis=0)
    dealt_rows = lax.all_to_all(dealt_acts, "req", split_axis=0, concat_axis=1, tiled=True).reshape(
        group_size, req_count, stretch_rows, features
    )
    gathered = lax.all_gather(dealt_rows, "head", axis=2, tiled=True)
    normed = (
        layer_norm(gathered.astype(jnp.float32), attn_gain)
        .astype(jnp.bfloat16)
        .reshape(group_size * stretch_max, features)
    )
    mixed = jnp.dot(
        normed,
        in_weight.reshape(features, heads_here * 3 * head_dim),
        preferred_element_type=jnp.float32,
    )
    mixed = mixed.reshape(group_size, stretch_max, heads_here, 3 * head_dim).astype(jnp.bfloat16)
    contexts = []
    for member in range(group_size):
        pairs = jnp.concatenate([current[member], mixed[member, :, :, head_dim:]], axis=0)
        contexts.append(
            attend(mixed[member, :, :, :head_dim], pairs, member_prefix[member], slopes, head_dim)
        )
    context = jnp.concatenate(contexts, axis=0)
    partial_attn = jnp.dot(
        context,
        out_weight.reshape(heads_here * head_dim, features),
        preferred_element_type=jnp.float32,
    )
    partial_attn = partial_attn.reshape(group_size, req_count, span_rows, features)
    attn_rows = head_sum(partial_attn, head_count, stretch_rows)
    residual_rows = dealt_rows.astype(jnp.float32) + attn_rows
    normed_rows = layer_norm(residual_rows, mlp_gain).astype(jnp.bfloat16)
    normed_all = head_gather(normed_rows, head_count)
    deferred, normed_all = lax.optimization_barrier((deferred, normed_all))
    for outgoing in deferred:
        chunks.append(land(lax.all_to_all(outgoing, ("req", "head"), 0, 0, tiled=True), req_count, head_count))
    relaid = jnp.stack(chunks, axis=1).reshape((req_count * local_layers,) + chunks[0].shape[1:])
    inner = jax.nn.gelu(
        jnp.dot(
            normed_all.reshape(group_size * stretch_max, features),
            up_weight,
            preferred_element_type=jnp.float32,
        ),
        approximate=False,
    ).astype(jnp.bfloat16)
    partial_mlp = jnp.dot(inner, down_weight, preferred_element_type=jnp.float32).reshape(
        group_size, req_count, span_rows, features
    )
    mlp_rows = head_sum(partial_mlp, head_count, stretch_rows)
    relaid, mlp_rows = lax.optimization_barrier((relaid, mlp_rows))
    row_number = (
        jnp.arange(req_count, dtype=jnp.int32)[:, None] * head_count + head_index
    ) * stretch_rows + jnp.arange(stretch_rows, dtype=jnp.int32)[None, :]
    usable = row_number[None] < member_stretch[:, None, None]
    result = jnp.where(
        usable[..., None], residual_rows + mlp_rows, jnp.zeros((), jnp.float32)
    ).astype(jnp.bfloat16)
    returned = lax.all_to_all(result, "req", split_axis=1, concat_axis=0, tiled=True).reshape(
        requests, stretch_rows, features
    )
    inverse = jnp.argsort(req_order)
    layer_out = jnp.take(returned, inverse, axis=0)
    return (layer_out, relaid)


def solution(mesh):
    return jax.shard_map(
        local,
        mesh=mesh,
        in_specs=(
            P(None, ("req", "head"), None),
            P("req", None, "head", None, None),
            P(),
            P(),
            P(),
            P(),
            P(None, "head", None),
            P("head"),
            P("head", None, None),
            P(),
            P(None, "head"),
            P("head", None),
        ),
        out_specs=(P(None, ("req", "head"), None), P(None, "req", None, "head", None)),
        check_vma=False,
    )
```

```python
import math

import jax
import jax.numpy as jnp
from jax import lax
from jax.sharding import PartitionSpec as P

EPSILON = 1e-05


def layer_norm(values, gain):
    average = jnp.mean(values, axis=-1, keepdims=True)
    centred = values - average
    variance = jnp.mean(centred * centred, axis=-1, keepdims=True)
    return centred * lax.rsqrt(variance + EPSILON) * gain.astype(jnp.float32)


def attend(queries, pairs, prefix_len, slopes, head_dim):
    stretch = queries.shape[0]
    prefix = pairs.shape[0] - stretch
    keys_part = pairs[..., :head_dim]
    values_part = pairs[..., head_dim:]
    scores = jnp.einsum("qhd,khd->hqk", queries, keys_part, preferred_element_type=jnp.float32) * (
        1.0 / math.sqrt(head_dim)
    )
    row_index = jnp.arange(stretch, dtype=jnp.int32)
    key_index = jnp.arange(prefix + stretch, dtype=jnp.int32)
    in_prefix = key_index < prefix
    query_pos = prefix_len + row_index
    key_pos = jnp.where(in_prefix, key_index, prefix_len + key_index - prefix)
    allowed = jnp.where(
        in_prefix[None, :],
        key_index[None, :] < prefix_len,
        (key_index - prefix)[None, :] <= row_index[:, None],
    )
    distance = (query_pos[:, None] - key_pos[None, :]).astype(jnp.float32)
    scores = scores - slopes[:, None, None] * distance[None]
    scores = jnp.where(allowed[None], scores, -jnp.inf)
    highest = jnp.max(scores, axis=-1, keepdims=True)
    expo = jnp.exp(scores - highest)
    soft = (expo / jnp.sum(expo, axis=-1, keepdims=True)).astype(jnp.bfloat16)
    context = jnp.einsum("hqk,khd->qhd", soft, values_part, preferred_element_type=jnp.float32)
    return context.astype(jnp.bfloat16).reshape(stretch, -1)


def head_sum(partial, head_count, stretch_rows):
    inner_size = 4 if head_count % 4 == 0 else head_count
    outer_size = head_count // inner_size
    me = lax.axis_index("head")
    outer_me, inner_me = me // inner_size, me % inner_size
    blocks = partial.astype(jnp.bfloat16).reshape(
        partial.shape[:2] + (outer_size, inner_size, stretch_rows) + partial.shape[3:]
    )
    level_one = lax.dynamic_index_in_dim(blocks, inner_me, 3, False).astype(jnp.float32)
    for shift in range(1, inner_size):
        pairs = [(j, (j // inner_size) * inner_size + (j % inner_size + shift) % inner_size) for j in range(head_count)]
        sent = lax.dynamic_index_in_dim(blocks, (inner_me + shift) % inner_size, 3, False)
        level_one = level_one + lax.ppermute(sent, "head", pairs).astype(jnp.float32)
    rounded_one = level_one.astype(jnp.bfloat16)
    total = lax.dynamic_index_in_dim(level_one, outer_me, 2, False)
    for shift in range(1, outer_size):
        pairs = [(j, ((j // inner_size + shift) % outer_size) * inner_size + j % inner_size) for j in range(head_count)]
        sent = lax.dynamic_index_in_dim(rounded_one, (outer_me + shift) % outer_size, 2, False)
        total = total + lax.ppermute(sent, "head", pairs).astype(jnp.float32)
    return total


def head_gather(rows, head_count):
    inner_size = 4 if head_count % 4 == 0 else head_count
    outer_size = head_count // inner_size
    me = lax.axis_index("head")
    outer_me, inner_me = me // inner_size, me % inner_size
    held = [rows]
    for shift in range(1, outer_size):
        pairs = [(j, ((j // inner_size + shift) % outer_size) * inner_size + j % inner_size) for j in range(head_count)]
        held.append(lax.ppermute(rows, "head", pairs))
    by_outer = jnp.take(jnp.stack(held), (outer_me - jnp.arange(outer_size)) % outer_size, axis=0)
    held = [by_outer]
    for shift in range(1, inner_size):
        pairs = [(j, (j // inner_size) * inner_size + (j % inner_size + shift) % inner_size) for j in range(head_count)]
        held.append(lax.ppermute(by_outer, "head", pairs))
    by_inner = jnp.take(jnp.stack(held), (inner_me - jnp.arange(inner_size)) % inner_size, axis=0)
    gathered = jnp.moveaxis(by_inner, (0, 1), (3, 2))
    return gathered.reshape(rows.shape[:2] + (head_count * rows.shape[2],) + rows.shape[3:])


def assemble(chunks, req_count, head_count):
    stacked = jnp.stack(chunks).reshape((len(chunks), req_count, head_count) + chunks[0].shape[1:])
    ordered = stacked.transpose(1, 0, 3, 2, 4, 5, 6)
    shape = ordered.shape
    return ordered.reshape((shape[0] * shape[1], shape[2], shape[3] * shape[4]) + shape[5:])


def land(incoming, req_count, head_count):
    shape = (req_count, head_count) + incoming.shape[1:]
    landed = incoming.reshape(shape).transpose(0, 2, 1, 3, 4, 5)
    return landed.reshape(landed.shape[:2] + (-1,) + landed.shape[4:])


def local(
    stretch_acts,
    cache_prefill,
    stretch_lens,
    prefix_lens,
    req_order,
    attn_gain,
    in_weight,
    slopes,
    out_weight,
    mlp_gain,
    up_weight,
    down_weight,
):
    req_count = lax.axis_size("req")
    head_count = lax.axis_size("head")
    req_index = lax.axis_index("req")
    head_index = lax.axis_index("head")
    requests = stretch_acts.shape[0]
    stretch_rows = stretch_acts.shape[1]
    features = stretch_acts.shape[2]
    group_size = requests // req_count
    span_rows = head_count * stretch_rows
    stretch_max = req_count * span_rows
    prefix_rows = cache_prefill.shape[2]
    heads_here = in_weight.shape[1]
    pair_width = cache_prefill.shape[4]
    head_dim = pair_width // 2
    members = lax.dynamic_slice_in_dim(req_order, req_index * group_size, group_size)
    member_stretch = jnp.take(stretch_lens, members)
    member_prefix = jnp.take(prefix_lens, members)
    ordered_prefix = jnp.take(prefix_lens, req_order)
    positions = head_index * prefix_rows + jnp.arange(prefix_rows, dtype=jnp.int32)
    keep = positions[None, :] < ordered_prefix[:, None]
    local_layers = cache_prefill.shape[0]
    slots = cache_prefill.shape[1]
    heads = cache_prefill.shape[3]
    devices = req_count * head_count
    chunks = []
    deferred = []
    later_layers = cache_prefill[1:]
    for layer in range(local_layers):
        source = cache_prefill[0] if layer == 0 else later_layers[layer - 1]
        dealt_cache = jnp.where(
            keep[:, :, None, None],
            jnp.take(source, req_order, axis=0),
            jnp.zeros((), cache_prefill.dtype),
        )
        outgoing = (
            dealt_cache.reshape(req_count, group_size, prefix_rows, head_count, heads // head_count, pair_width)
            .transpose(0, 3, 1, 2, 4, 5)
            .reshape(devices, group_size, prefix_rows, heads // head_count, pair_width)
        )
        if layer == 0:
            incoming = lax.all_to_all(outgoing, ("req", "head"), 0, 0, tiled=True)
            incoming, later_layers = lax.optimization_barrier((incoming, later_layers))
            chunks.append(incoming)
        else:
            deferred.append(outgoing)
    current = land(chunks[0][:head_count], 1, head_count)[0]
    dealt_acts = jnp.take(stretch_acts, req_order, axis=0)
    dealt_rows = lax.all_to_all(dealt_acts, "req", split_axis=0, concat_axis=1, tiled=True).reshape(
        group_size, req_count, stretch_rows, features
    )
    gathered = lax.all_gather(dealt_rows, "head", axis=2, tiled=True)
    normed = (
        layer_norm(gathered.astype(jnp.float32), attn_gain)
        .astype(jnp.bfloat16)
        .reshape(group_size * stretch_max, features)
    )
    mixed = jnp.dot(
        normed,
        in_weight.reshape(features, heads_here * 3 * head_dim),
        preferred_element_type=jnp.float32,
    )
    mixed = mixed.reshape(group_size, stretch_max, heads_here, 3 * head_dim).astype(jnp.bfloat16)
    contexts = []
    for member in range(group_size):
        pairs = jnp.concatenate([current[member], mixed[member, :, :, head_dim:]], axis=0)
        contexts.append(
            attend(mixed[member, :, :, :head_dim], pairs, member_prefix[member], slopes, head_dim)
        )
    context = jnp.concatenate(contexts, axis=0)
    partial_attn = jnp.dot(
        context,
        out_weight.reshape(heads_here * head_dim, features),
        preferred_element_type=jnp.float32,
    )
    partial_attn = partial_attn.reshape(group_size, req_count, span_rows, features)
    attn_rows = head_sum(partial_attn, head_count, stretch_rows)
    residual_rows = dealt_rows.astype(jnp.float32) + attn_rows
    normed_rows = layer_norm(residual_rows, mlp_gain).astype(jnp.bfloat16)
    normed_all = head_gather(normed_rows, head_count)
    deferred, normed_all = lax.optimization_barrier((deferred, normed_all))
    for outgoing in deferred:
        chunks.append(lax.all_to_all(outgoing, ("req", "head"), 0, 0, tiled=True))
    relaid = assemble(chunks, req_count, head_count)
    inner = jax.nn.gelu(
        jnp.dot(
            normed_all.reshape(group_size * stretch_max, features),
            up_weight,
            preferred_element_type=jnp.float32,
        ),
        approximate=False,
    ).astype(jnp.bfloat16)
    partial_mlp = jnp.dot(inner, down_weight, preferred_element_type=jnp.float32).reshape(
        group_size, req_count, span_rows, features
    )
    mlp_rows = head_sum(partial_mlp, head_count, stretch_rows)
    row_number = (
        jnp.arange(req_count, dtype=jnp.int32)[:, None] * head_count + head_index
    ) * stretch_rows + jnp.arange(stretch_rows, dtype=jnp.int32)[None, :]
    usable = row_number[None] < member_stretch[:, None, None]
    result = jnp.where(
        usable[..., None], residual_rows + mlp_rows, jnp.zeros((), jnp.float32)
    ).astype(jnp.bfloat16)
    returned = lax.all_to_all(result, "req", split_axis=1, concat_axis=0, tiled=True).reshape(
        requests, stretch_rows, features
    )
    inverse = jnp.argsort(req_order)
    layer_out = jnp.take(returned, inverse, axis=0)
    return (layer_out, relaid)


def solution(mesh):
    return jax.shard_map(
        local,
        mesh=mesh,
        in_specs=(
            P(None, ("req", "head"), None),
            P("req", None, "head", None, None),
            P(),
            P(),
            P(),
            P(),
            P(None, "head", None),
            P("head"),
            P("head", None, None),
            P(),
            P(None, "head"),
            P("head", None),
        ),
        out_specs=(P(None, ("req", "head"), None), P(None, "req", None, "head", None)),
        check_vma=False,
    )
```

```python
import math

import jax
import jax.numpy as jnp
from jax import lax
from jax.sharding import PartitionSpec as P

EPSILON = 1e-05


def layer_norm(values, gain):
    average = jnp.mean(values, axis=-1, keepdims=True)
    centred = values - average
    variance = jnp.mean(centred * centred, axis=-1, keepdims=True)
    return centred * lax.rsqrt(variance + EPSILON) * gain.astype(jnp.float32)


def attend(queries, pairs, prefix_len, slopes, head_dim):
    stretch = queries.shape[0]
    prefix = pairs.shape[0] - stretch
    keys_part = pairs[..., :head_dim]
    values_part = pairs[..., head_dim:]
    scores = jnp.einsum("qhd,khd->hqk", queries, keys_part, preferred_element_type=jnp.float32) * (
        1.0 / math.sqrt(head_dim)
    )
    row_index = jnp.arange(stretch, dtype=jnp.int32)
    key_index = jnp.arange(prefix + stretch, dtype=jnp.int32)
    in_prefix = key_index < prefix
    query_pos = prefix_len + row_index
    key_pos = jnp.where(in_prefix, key_index, prefix_len + key_index - prefix)
    allowed = jnp.where(
        in_prefix[None, :],
        key_index[None, :] < prefix_len,
        (key_index - prefix)[None, :] <= row_index[:, None],
    )
    distance = (query_pos[:, None] - key_pos[None, :]).astype(jnp.float32)
    scores = scores - slopes[:, None, None] * distance[None]
    scores = jnp.where(allowed[None], scores, -jnp.inf)
    highest = jnp.max(scores, axis=-1, keepdims=True)
    expo = jnp.exp(scores - highest)
    soft = (expo / jnp.sum(expo, axis=-1, keepdims=True)).astype(jnp.bfloat16)
    context = jnp.einsum("hqk,khd->qhd", soft, values_part, preferred_element_type=jnp.float32)
    return context.astype(jnp.bfloat16).reshape(stretch, -1)


def head_sum(partial, head_count, stretch_rows):
    inner_size = 4 if head_count % 4 == 0 else head_count
    outer_size = head_count // inner_size
    me = lax.axis_index("head")
    outer_me, inner_me = me // inner_size, me % inner_size
    blocks = partial.astype(jnp.bfloat16).reshape(
        partial.shape[:2] + (outer_size, inner_size, stretch_rows) + partial.shape[3:]
    )
    level_one = lax.dynamic_index_in_dim(blocks, inner_me, 3, False).astype(jnp.float32)
    for shift in range(1, inner_size):
        pairs = [(j, (j // inner_size) * inner_size + (j % inner_size + shift) % inner_size) for j in range(head_count)]
        sent = lax.dynamic_index_in_dim(blocks, (inner_me + shift) % inner_size, 3, False)
        level_one = level_one + lax.ppermute(sent, "head", pairs).astype(jnp.float32)
    rounded_one = level_one.astype(jnp.bfloat16)
    total = lax.dynamic_index_in_dim(level_one, outer_me, 2, False)
    for shift in range(1, outer_size):
        pairs = [(j, ((j // inner_size + shift) % outer_size) * inner_size + j % inner_size) for j in range(head_count)]
        sent = lax.dynamic_index_in_dim(rounded_one, (outer_me + shift) % outer_size, 2, False)
        total = total + lax.ppermute(sent, "head", pairs).astype(jnp.float32)
    return total


def head_gather(rows, head_count):
    inner_size = 4 if head_count % 4 == 0 else head_count
    outer_size = head_count // inner_size
    me = lax.axis_index("head")
    outer_me, inner_me = me // inner_size, me % inner_size
    held = [rows]
    for shift in range(1, outer_size):
        pairs = [(j, ((j // inner_size + shift) % outer_size) * inner_size + j % inner_size) for j in range(head_count)]
        held.append(lax.ppermute(rows, "head", pairs))
    by_outer = jnp.take(jnp.stack(held), (outer_me - jnp.arange(outer_size)) % outer_size, axis=0)
    held = [by_outer]
    for shift in range(1, inner_size):
        pairs = [(j, (j // inner_size) * inner_size + (j % inner_size + shift) % inner_size) for j in range(head_count)]
        held.append(lax.ppermute(by_outer, "head", pairs))
    by_inner = jnp.take(jnp.stack(held), (inner_me - jnp.arange(inner_size)) % inner_size, axis=0)
    gathered = jnp.moveaxis(by_inner, (0, 1), (3, 2))
    return gathered.reshape(rows.shape[:2] + (head_count * rows.shape[2],) + rows.shape[3:])


def assemble(chunks, req_count, head_count):
    stacked = jnp.stack(chunks).reshape((len(chunks), req_count, head_count) + chunks[0].shape[1:])
    ordered = stacked.transpose(1, 0, 3, 2, 4, 5, 6)
    shape = ordered.shape
    return ordered.reshape((shape[0] * shape[1], shape[2], shape[3] * shape[4]) + shape[5:])


def land(incoming, req_count, head_count):
    shape = (req_count, head_count) + incoming.shape[1:]
    landed = incoming.reshape(shape).transpose(0, 2, 1, 3, 4, 5)
    return landed.reshape(landed.shape[:2] + (-1,) + landed.shape[4:])


def local(
    stretch_acts,
    cache_prefill,
    stretch_lens,
    prefix_lens,
    req_order,
    attn_gain,
    in_weight,
    slopes,
    out_weight,
    mlp_gain,
    up_weight,
    down_weight,
):
    req_count = lax.axis_size("req")
    head_count = lax.axis_size("head")
    req_index = lax.axis_index("req")
    head_index = lax.axis_index("head")
    requests = stretch_acts.shape[0]
    stretch_rows = stretch_acts.shape[1]
    features = stretch_acts.shape[2]
    group_size = requests // req_count
    span_rows = head_count * stretch_rows
    stretch_max = req_count * span_rows
    prefix_rows = cache_prefill.shape[2]
    heads_here = in_weight.shape[1]
    pair_width = cache_prefill.shape[4]
    head_dim = pair_width // 2
    members = lax.dynamic_slice_in_dim(req_order, req_index * group_size, group_size)
    member_stretch = jnp.take(stretch_lens, members)
    member_prefix = jnp.take(prefix_lens, members)
    ordered_prefix = jnp.take(prefix_lens, req_order)
    positions = head_index * prefix_rows + jnp.arange(prefix_rows, dtype=jnp.int32)
    keep = positions[None, :] < ordered_prefix[:, None]
    local_layers = cache_prefill.shape[0]
    slots = cache_prefill.shape[1]
    heads = cache_prefill.shape[3]
    devices = req_count * head_count
    chunks = []
    deferred = []
    later_layers = cache_prefill[1:]
    for layer in range(local_layers):
        source = cache_prefill[0] if layer == 0 else later_layers[layer - 1]
        dealt_cache = jnp.where(
            keep[:, :, None, None],
            jnp.take(source, req_order, axis=0),
            jnp.zeros((), cache_prefill.dtype),
        )
        outgoing = (
            dealt_cache.reshape(req_count, group_size, prefix_rows, head_count, heads // head_count, pair_width)
            .transpose(0, 3, 1, 2, 4, 5)
            .reshape(devices, group_size, prefix_rows, heads // head_count, pair_width)
        )
        if layer == 0:
            incoming = lax.all_to_all(outgoing, ("req", "head"), 0, 0, tiled=True)
            incoming, later_layers = lax.optimization_barrier((incoming, later_layers))
            chunks.append(incoming)
        else:
            deferred.append(outgoing)
    current = land(chunks[0][:head_count], 1, head_count)[0]
    dealt_acts = jnp.take(stretch_acts, req_order, axis=0)
    dealt_rows = lax.all_to_all(dealt_acts, "req", split_axis=0, concat_axis=1, tiled=True).reshape(
        group_size, req_count, stretch_rows, features
    )
    gathered = lax.all_gather(dealt_rows, "head", axis=2, tiled=True)
    normed = (
        layer_norm(gathered.astype(jnp.float32), attn_gain)
        .astype(jnp.bfloat16)
        .reshape(group_size * stretch_max, features)
    )
    mixed = jnp.dot(
        normed,
        in_weight.reshape(features, heads_here * 3 * head_dim),
        preferred_element_type=jnp.float32,
    )
    mixed = mixed.reshape(group_size, stretch_max, heads_here, 3 * head_dim).astype(jnp.bfloat16)
    contexts = []
    for member in range(group_size):
        pairs = jnp.concatenate([current[member], mixed[member, :, :, head_dim:]], axis=0)
        contexts.append(
            attend(mixed[member, :, :, :head_dim], pairs, member_prefix[member], slopes, head_dim)
        )
    context = jnp.concatenate(contexts, axis=0)
    partial_attn = jnp.dot(
        context,
        out_weight.reshape(heads_here * head_dim, features),
        preferred_element_type=jnp.float32,
    )
    partial_attn = partial_attn.reshape(group_size, req_count, span_rows, features)
    attn_rows = head_sum(partial_attn, head_count, stretch_rows)
    residual_rows = dealt_rows.astype(jnp.float32) + attn_rows
    normed_rows = layer_norm(residual_rows, mlp_gain).astype(jnp.bfloat16)
    normed_all = head_gather(normed_rows, head_count)
    deferred, normed_all = lax.optimization_barrier((deferred, normed_all))
    for outgoing in deferred:
        chunks.append(lax.all_to_all(outgoing, ("req", "head"), 0, 0, tiled=True))
    relaid = assemble(chunks, req_count, head_count)
    inner = jax.nn.gelu(
        jnp.dot(
            normed_all.reshape(group_size * stretch_max, features),
            up_weight,
            preferred_element_type=jnp.float32,
        ),
        approximate=False,
    ).astype(jnp.bfloat16)
    partial_mlp = jnp.dot(inner, down_weight, preferred_element_type=jnp.float32).reshape(
        group_size, req_count, span_rows, features
    )
    mlp_rows = head_sum(partial_mlp, head_count, stretch_rows)
    relaid, mlp_rows = lax.optimization_barrier((relaid, mlp_rows))
    row_number = (
        jnp.arange(req_count, dtype=jnp.int32)[:, None] * head_count + head_index
    ) * stretch_rows + jnp.arange(stretch_rows, dtype=jnp.int32)[None, :]
    usable = row_number[None] < member_stretch[:, None, None]
    result = jnp.where(
        usable[..., None], residual_rows + mlp_rows, jnp.zeros((), jnp.float32)
    ).astype(jnp.bfloat16)
    returned = lax.all_to_all(result, "req", split_axis=1, concat_axis=0, tiled=True).reshape(
        requests, stretch_rows, features
    )
    inverse = jnp.argsort(req_order)
    layer_out = jnp.take(returned, inverse, axis=0)
    return (layer_out, relaid)


def solution(mesh):
    return jax.shard_map(
        local,
        mesh=mesh,
        in_specs=(
            P(None, ("req", "head"), None),
            P("req", None, "head", None, None),
            P(),
            P(),
            P(),
            P(),
            P(None, "head", None),
            P("head"),
            P("head", None, None),
            P(),
            P(None, "head"),
            P("head", None),
        ),
        out_specs=(P(None, ("req", "head"), None), P(None, "req", None, "head", None)),
        check_vma=False,
    )
```

```python
import math

import jax
import jax.numpy as jnp
from jax import lax
from jax.sharding import PartitionSpec as P

EPSILON = 1e-05


def layer_norm(values, gain):
    average = jnp.mean(values, axis=-1, keepdims=True)
    centred = values - average
    variance = jnp.mean(centred * centred, axis=-1, keepdims=True)
    return centred * lax.rsqrt(variance + EPSILON) * gain.astype(jnp.float32)


def attend(queries, pairs, prefix_len, slopes, head_dim):
    stretch = queries.shape[0]
    prefix = pairs.shape[0] - stretch
    keys_part = pairs[..., :head_dim]
    values_part = pairs[..., head_dim:]
    scores = jnp.einsum("qhd,khd->hqk", queries, keys_part, preferred_element_type=jnp.float32) * (
        1.0 / math.sqrt(head_dim)
    )
    row_index = jnp.arange(stretch, dtype=jnp.int32)
    key_index = jnp.arange(prefix + stretch, dtype=jnp.int32)
    in_prefix = key_index < prefix
    query_pos = prefix_len + row_index
    key_pos = jnp.where(in_prefix, key_index, prefix_len + key_index - prefix)
    allowed = jnp.where(
        in_prefix[None, :],
        key_index[None, :] < prefix_len,
        (key_index - prefix)[None, :] <= row_index[:, None],
    )
    distance = (query_pos[:, None] - key_pos[None, :]).astype(jnp.float32)
    scores = scores - slopes[:, None, None] * distance[None]
    scores = jnp.where(allowed[None], scores, -jnp.inf)
    highest = jnp.max(scores, axis=-1, keepdims=True)
    expo = jnp.exp(scores - highest)
    soft = (expo / jnp.sum(expo, axis=-1, keepdims=True)).astype(jnp.bfloat16)
    context = jnp.einsum("hqk,khd->qhd", soft, values_part, preferred_element_type=jnp.float32)
    return context.astype(jnp.bfloat16).reshape(stretch, -1)


def head_sum(partial, head_count, stretch_rows):
    inner_size = 4 if head_count % 4 == 0 else head_count
    outer_size = head_count // inner_size
    me = lax.axis_index("head")
    outer_me, inner_me = me // inner_size, me % inner_size
    blocks = partial.astype(jnp.bfloat16).reshape(
        partial.shape[:2] + (outer_size, inner_size, stretch_rows) + partial.shape[3:]
    )
    level_one = lax.dynamic_index_in_dim(blocks, inner_me, 3, False).astype(jnp.float32)
    for shift in range(1, inner_size):
        pairs = [(j, (j // inner_size) * inner_size + (j % inner_size + shift) % inner_size) for j in range(head_count)]
        sent = lax.dynamic_index_in_dim(blocks, (inner_me + shift) % inner_size, 3, False)
        level_one = level_one + lax.ppermute(sent, "head", pairs).astype(jnp.float32)
    rounded_one = level_one.astype(jnp.bfloat16)
    total = lax.dynamic_index_in_dim(level_one, outer_me, 2, False)
    for shift in range(1, outer_size):
        pairs = [(j, ((j // inner_size + shift) % outer_size) * inner_size + j % inner_size) for j in range(head_count)]
        sent = lax.dynamic_index_in_dim(rounded_one, (outer_me + shift) % outer_size, 2, False)
        total = total + lax.ppermute(sent, "head", pairs).astype(jnp.float32)
    return total


def head_gather(rows, head_count):
    inner_size = 4 if head_count % 4 == 0 else head_count
    outer_size = head_count // inner_size
    me = lax.axis_index("head")
    outer_me, inner_me = me // inner_size, me % inner_size
    held = [rows]
    for shift in range(1, outer_size):
        pairs = [(j, ((j // inner_size + shift) % outer_size) * inner_size + j % inner_size) for j in range(head_count)]
        held.append(lax.ppermute(rows, "head", pairs))
    by_outer = jnp.take(jnp.stack(held), (outer_me - jnp.arange(outer_size)) % outer_size, axis=0)
    held = [by_outer]
    for shift in range(1, inner_size):
        pairs = [(j, (j // inner_size) * inner_size + (j % inner_size + shift) % inner_size) for j in range(head_count)]
        held.append(lax.ppermute(by_outer, "head", pairs))
    by_inner = jnp.take(jnp.stack(held), (inner_me - jnp.arange(inner_size)) % inner_size, axis=0)
    gathered = jnp.moveaxis(by_inner, (0, 1), (3, 2))
    return gathered.reshape(rows.shape[:2] + (head_count * rows.shape[2],) + rows.shape[3:])


def land(incoming, req_count, head_count):
    shape = (req_count, head_count) + incoming.shape[1:]
    landed = incoming.reshape(shape).transpose(0, 2, 1, 3, 4, 5)
    return landed.reshape(landed.shape[:2] + (-1,) + landed.shape[4:])


def req_exchange(dealt_acts, req_count):
    me = lax.axis_index("req")
    blocks = dealt_acts.reshape((req_count, -1) + dealt_acts.shape[1:])
    held = [lax.dynamic_index_in_dim(blocks, me, 0, False)]
    for shift in range(1, req_count):
        pairs = [(a, (a + shift) % req_count) for a in range(req_count)]
        held.append(lax.ppermute(lax.dynamic_index_in_dim(blocks, (me + shift) % req_count, 0, False), "req", pairs))
    ordered = jnp.take(jnp.stack(held), (me - jnp.arange(req_count)) % req_count, axis=0)
    return ordered.transpose(1, 0, 2, 3)


def local(
    stretch_acts,
    cache_prefill,
    stretch_lens,
    prefix_lens,
    req_order,
    attn_gain,
    in_weight,
    slopes,
    out_weight,
    mlp_gain,
    up_weight,
    down_weight,
):
    req_count = lax.axis_size("req")
    head_count = lax.axis_size("head")
    req_index = lax.axis_index("req")
    head_index = lax.axis_index("head")
    requests = stretch_acts.shape[0]
    stretch_rows = stretch_acts.shape[1]
    features = stretch_acts.shape[2]
    group_size = requests // req_count
    span_rows = head_count * stretch_rows
    stretch_max = req_count * span_rows
    prefix_rows = cache_prefill.shape[2]
    heads_here = in_weight.shape[1]
    pair_width = cache_prefill.shape[4]
    head_dim = pair_width // 2
    members = lax.dynamic_slice_in_dim(req_order, req_index * group_size, group_size)
    member_stretch = jnp.take(stretch_lens, members)
    member_prefix = jnp.take(prefix_lens, members)
    ordered_prefix = jnp.take(prefix_lens, req_order)
    positions = head_index * prefix_rows + jnp.arange(prefix_rows, dtype=jnp.int32)
    keep = positions[None, :] < ordered_prefix[:, None]
    local_layers = cache_prefill.shape[0]
    slots = cache_prefill.shape[1]
    heads = cache_prefill.shape[3]
    devices = req_count * head_count
    chunks = []
    deferred = []
    later_layers = cache_prefill[1:]
    for layer in range(local_layers):
        source = cache_prefill[0] if layer == 0 else later_layers[layer - 1]
        dealt_cache = jnp.where(
            keep[:, :, None, None],
            jnp.take(source, req_order, axis=0),
            jnp.zeros((), cache_prefill.dtype),
        )
        outgoing = (
            dealt_cache.reshape(req_count, group_size, prefix_rows, head_count, heads // head_count, pair_width)
            .transpose(0, 3, 1, 2, 4, 5)
            .reshape(devices, group_size, prefix_rows, heads // head_count, pair_width)
        )
        if layer == 0:
            incoming = lax.all_to_all(outgoing, ("req", "head"), 0, 0, tiled=True)
            incoming, later_layers = lax.optimization_barrier((incoming, later_layers))
            chunks.append(land(incoming, req_count, head_count))
        else:
            deferred.append(outgoing)
    current = chunks[0][0]
    dealt_acts = jnp.take(stretch_acts, req_order, axis=0)
    dealt_rows = req_exchange(dealt_acts, req_count)
    gathered = lax.all_gather(dealt_rows, "head", axis=2, tiled=True)
    normed = (
        layer_norm(gathered.astype(jnp.float32), attn_gain)
        .astype(jnp.bfloat16)
        .reshape(group_size * stretch_max, features)
    )
    mixed = jnp.dot(
        normed,
        in_weight.reshape(features, heads_here * 3 * head_dim),
        preferred_element_type=jnp.float32,
    )
    mixed = mixed.reshape(group_size, stretch_max, heads_here, 3 * head_dim).astype(jnp.bfloat16)
    contexts = []
    for member in range(group_size):
        pairs = jnp.concatenate([current[member], mixed[member, :, :, head_dim:]], axis=0)
        contexts.append(
            attend(mixed[member, :, :, :head_dim], pairs, member_prefix[member], slopes, head_dim)
        )
    context = jnp.concatenate(contexts, axis=0)
    partial_attn = jnp.dot(
        context,
        out_weight.reshape(heads_here * head_dim, features),
        preferred_element_type=jnp.float32,
    )
    partial_attn = partial_attn.reshape(group_size, req_count, span_rows, features)
    attn_rows = head_sum(partial_attn, head_count, stretch_rows)
    residual_rows = dealt_rows.astype(jnp.float32) + attn_rows
    normed_rows = layer_norm(residual_rows, mlp_gain).astype(jnp.bfloat16)
    normed_all = head_gather(normed_rows, head_count)
    deferred, normed_all = lax.optimization_barrier((deferred, normed_all))
    for outgoing in deferred:
        chunks.append(land(lax.all_to_all(outgoing, ("req", "head"), 0, 0, tiled=True), req_count, head_count))
    relaid = jnp.stack(chunks, axis=1).reshape((req_count * local_layers,) + chunks[0].shape[1:])
    inner = jax.nn.gelu(
        jnp.dot(
            normed_all.reshape(group_size * stretch_max, features),
            up_weight,
            preferred_element_type=jnp.float32,
        ),
        approximate=False,
    ).astype(jnp.bfloat16)
    partial_mlp = jnp.dot(inner, down_weight, preferred_element_type=jnp.float32).reshape(
        group_size, req_count, span_rows, features
    )
    mlp_rows = head_sum(partial_mlp, head_count, stretch_rows)
    relaid, mlp_rows = lax.optimization_barrier((relaid, mlp_rows))
    row_number = (
        jnp.arange(req_count, dtype=jnp.int32)[:, None] * head_count + head_index
    ) * stretch_rows + jnp.arange(stretch_rows, dtype=jnp.int32)[None, :]
    usable = row_number[None] < member_stretch[:, None, None]
    result = jnp.where(
        usable[..., None], residual_rows + mlp_rows, jnp.zeros((), jnp.float32)
    ).astype(jnp.bfloat16)
    returned = lax.all_to_all(result, "req", split_axis=1, concat_axis=0, tiled=True).reshape(
        requests, stretch_rows, features
    )
    inverse = jnp.argsort(req_order)
    layer_out = jnp.take(returned, inverse, axis=0)
    return (layer_out, relaid)


def solution(mesh):
    return jax.shard_map(
        local,
        mesh=mesh,
        in_specs=(
            P(None, ("req", "head"), None),
            P("req", None, "head", None, None),
            P(),
            P(),
            P(),
            P(),
            P(None, "head", None),
            P("head"),
            P("head", None, None),
            P(),
            P(None, "head"),
            P("head", None),
        ),
        out_specs=(P(None, ("req", "head"), None), P(None, "req", None, "head", None)),
        check_vma=False,
    )
```

```python
import math

import jax
import jax.numpy as jnp
from jax import lax
from jax.sharding import PartitionSpec as P

EPSILON = 1e-05


def layer_norm(values, gain):
    average = jnp.mean(values, axis=-1, keepdims=True)
    centred = values - average
    variance = jnp.mean(centred * centred, axis=-1, keepdims=True)
    return centred * lax.rsqrt(variance + EPSILON) * gain.astype(jnp.float32)


def attend(queries, pairs, prefix_len, slopes, head_dim):
    stretch = queries.shape[0]
    prefix = pairs.shape[0] - stretch
    keys_part = pairs[..., :head_dim]
    values_part = pairs[..., head_dim:]
    scores = jnp.einsum("qhd,khd->hqk", queries, keys_part, preferred_element_type=jnp.float32) * (
        1.0 / math.sqrt(head_dim)
    )
    row_index = jnp.arange(stretch, dtype=jnp.int32)
    key_index = jnp.arange(prefix + stretch, dtype=jnp.int32)
    in_prefix = key_index < prefix
    query_pos = prefix_len + row_index
    key_pos = jnp.where(in_prefix, key_index, prefix_len + key_index - prefix)
    allowed = jnp.where(
        in_prefix[None, :],
        key_index[None, :] < prefix_len,
        (key_index - prefix)[None, :] <= row_index[:, None],
    )
    distance = (query_pos[:, None] - key_pos[None, :]).astype(jnp.float32)
    scores = scores - slopes[:, None, None] * distance[None]
    scores = jnp.where(allowed[None], scores, -jnp.inf)
    highest = jnp.max(scores, axis=-1, keepdims=True)
    expo = jnp.exp(scores - highest)
    soft = (expo / jnp.sum(expo, axis=-1, keepdims=True)).astype(jnp.bfloat16)
    context = jnp.einsum("hqk,khd->qhd", soft, values_part, preferred_element_type=jnp.float32)
    return context.astype(jnp.bfloat16).reshape(stretch, -1)


def head_sum(partial, head_count, stretch_rows):
    inner_size = 4 if head_count % 4 == 0 else head_count
    outer_size = head_count // inner_size
    me = lax.axis_index("head")
    outer_me, inner_me = me // inner_size, me % inner_size
    blocks = partial.astype(jnp.bfloat16).reshape(
        partial.shape[:2] + (outer_size, inner_size, stretch_rows) + partial.shape[3:]
    )
    level_one = lax.dynamic_index_in_dim(blocks, inner_me, 3, False).astype(jnp.float32)
    for shift in range(1, inner_size):
        pairs = [(j, (j // inner_size) * inner_size + (j % inner_size + shift) % inner_size) for j in range(head_count)]
        sent = lax.dynamic_index_in_dim(blocks, (inner_me + shift) % inner_size, 3, False)
        level_one = level_one + lax.ppermute(sent, "head", pairs).astype(jnp.float32)
    rounded_one = level_one.astype(jnp.bfloat16)
    total = lax.dynamic_index_in_dim(level_one, outer_me, 2, False)
    for shift in range(1, outer_size):
        pairs = [(j, ((j // inner_size + shift) % outer_size) * inner_size + j % inner_size) for j in range(head_count)]
        sent = lax.dynamic_index_in_dim(rounded_one, (outer_me + shift) % outer_size, 2, False)
        total = total + lax.ppermute(sent, "head", pairs).astype(jnp.float32)
    return total


def head_gather(rows, head_count):
    inner_size = 4 if head_count % 4 == 0 else head_count
    outer_size = head_count // inner_size
    me = lax.axis_index("head")
    outer_me, inner_me = me // inner_size, me % inner_size
    held = [rows]
    for shift in range(1, outer_size):
        pairs = [(j, ((j // inner_size + shift) % outer_size) * inner_size + j % inner_size) for j in range(head_count)]
        held.append(lax.ppermute(rows, "head", pairs))
    by_outer = jnp.take(jnp.stack(held), (outer_me - jnp.arange(outer_size)) % outer_size, axis=0)
    held = [by_outer]
    for shift in range(1, inner_size):
        pairs = [(j, (j // inner_size) * inner_size + (j % inner_size + shift) % inner_size) for j in range(head_count)]
        held.append(lax.ppermute(by_outer, "head", pairs))
    by_inner = jnp.take(jnp.stack(held), (inner_me - jnp.arange(inner_size)) % inner_size, axis=0)
    gathered = jnp.moveaxis(by_inner, (0, 1), (3, 2))
    return gathered.reshape(rows.shape[:2] + (head_count * rows.shape[2],) + rows.shape[3:])


def land(incoming, req_count, head_count):
    shape = (req_count, head_count) + incoming.shape[1:]
    landed = incoming.reshape(shape).transpose(0, 2, 1, 3, 4, 5)
    return landed.reshape(landed.shape[:2] + (-1,) + landed.shape[4:])


def local(
    stretch_acts,
    cache_prefill,
    stretch_lens,
    prefix_lens,
    req_order,
    attn_gain,
    in_weight,
    slopes,
    out_weight,
    mlp_gain,
    up_weight,
    down_weight,
):
    req_count = lax.axis_size("req")
    head_count = lax.axis_size("head")
    req_index = lax.axis_index("req")
    head_index = lax.axis_index("head")
    requests = stretch_acts.shape[0]
    stretch_rows = stretch_acts.shape[1]
    features = stretch_acts.shape[2]
    group_size = requests // req_count
    span_rows = head_count * stretch_rows
    stretch_max = req_count * span_rows
    prefix_rows = cache_prefill.shape[2]
    heads_here = in_weight.shape[1]
    pair_width = cache_prefill.shape[4]
    head_dim = pair_width // 2
    members = lax.dynamic_slice_in_dim(req_order, req_index * group_size, group_size)
    member_stretch = jnp.take(stretch_lens, members)
    member_prefix = jnp.take(prefix_lens, members)
    ordered_prefix = jnp.take(prefix_lens, req_order)
    positions = head_index * prefix_rows + jnp.arange(prefix_rows, dtype=jnp.int32)
    keep = positions[None, :] < ordered_prefix[:, None]
    local_layers = cache_prefill.shape[0]
    slots = cache_prefill.shape[1]
    heads = cache_prefill.shape[3]
    devices = req_count * head_count
    chunks = []
    deferred = []
    later_layers = cache_prefill[1:]
    for layer in range(local_layers):
        source = cache_prefill[0] if layer == 0 else later_layers[layer - 1]
        dealt_cache = jnp.where(
            keep[:, :, None, None],
            jnp.take(source, req_order, axis=0),
            jnp.zeros((), cache_prefill.dtype),
        )
        outgoing = (
            dealt_cache.reshape(req_count, group_size, prefix_rows, head_count, heads // head_count, pair_width)
            .transpose(0, 3, 1, 2, 4, 5)
            .reshape(devices, group_size, prefix_rows, heads // head_count, pair_width)
        )
        if layer == 0:
            incoming = lax.all_to_all(outgoing, ("req", "head"), 0, 0, tiled=True)
            incoming, later_layers = lax.optimization_barrier((incoming, later_layers))
            chunks.append(land(incoming, req_count, head_count))
        else:
            deferred.append(outgoing)
    current = chunks[0][0]
    dealt_acts = jnp.take(stretch_acts, req_order, axis=0)
    dealt_rows = lax.all_to_all(dealt_acts, "req", split_axis=0, concat_axis=1, tiled=True).reshape(
        group_size, req_count, stretch_rows, features
    )
    gathered = lax.all_gather(dealt_rows, "head", axis=2, tiled=True)
    normed = (
        layer_norm(gathered.astype(jnp.float32), attn_gain)
        .astype(jnp.bfloat16)
        .reshape(group_size * stretch_max, features)
    )
    mixed = jnp.dot(
        normed,
        in_weight.reshape(features, heads_here * 3 * head_dim),
        preferred_element_type=jnp.float32,
    )
    mixed = mixed.reshape(group_size, stretch_max, heads_here, 3 * head_dim).astype(jnp.bfloat16)
    contexts = []
    for member in range(group_size):
        pairs = jnp.concatenate([current[member], mixed[member, :, :, head_dim:]], axis=0)
        contexts.append(
            attend(mixed[member, :, :, :head_dim], pairs, member_prefix[member], slopes, head_dim)
        )
    context = jnp.concatenate(contexts, axis=0)
    partial_attn = jnp.dot(
        context,
        out_weight.reshape(heads_here * head_dim, features),
        preferred_element_type=jnp.float32,
    )
    partial_attn = partial_attn.reshape(group_size, req_count, span_rows, features)
    attn_rows = head_sum(partial_attn, head_count, stretch_rows)
    residual_rows = dealt_rows.astype(jnp.float32) + attn_rows
    normed_rows = layer_norm(residual_rows, mlp_gain).astype(jnp.bfloat16)
    normed_all = head_gather(normed_rows, head_count)
    deferred, normed_all = lax.optimization_barrier((deferred, normed_all))
    for outgoing in deferred:
        chunks.append(land(lax.all_to_all(outgoing, ("req", "head"), 0, 0, tiled=True), req_count, head_count))
    relaid = jnp.stack(chunks, axis=1).reshape((req_count * local_layers,) + chunks[0].shape[1:])
    member_sums = []
    for member in range(group_size):
        inner = jax.nn.gelu(
            jnp.dot(
                normed_all[member].reshape(stretch_max, features),
                up_weight,
                preferred_element_type=jnp.float32,
            ),
            approximate=False,
        ).astype(jnp.bfloat16)
        partial_mlp = jnp.dot(inner, down_weight, preferred_element_type=jnp.float32).reshape(
            1, req_count, span_rows, features
        )
        member_sums.append(head_sum(partial_mlp, head_count, stretch_rows))
    mlp_rows = jnp.concatenate(member_sums, axis=0)
    relaid, mlp_rows = lax.optimization_barrier((relaid, mlp_rows))
    row_number = (
        jnp.arange(req_count, dtype=jnp.int32)[:, None] * head_count + head_index
    ) * stretch_rows + jnp.arange(stretch_rows, dtype=jnp.int32)[None, :]
    usable = row_number[None] < member_stretch[:, None, None]
    result = jnp.where(
        usable[..., None], residual_rows + mlp_rows, jnp.zeros((), jnp.float32)
    ).astype(jnp.bfloat16)
    returned = lax.all_to_all(result, "req", split_axis=1, concat_axis=0, tiled=True).reshape(
        requests, stretch_rows, features
    )
    inverse = jnp.argsort(req_order)
    layer_out = jnp.take(returned, inverse, axis=0)
    return (layer_out, relaid)


def solution(mesh):
    return jax.shard_map(
        local,
        mesh=mesh,
        in_specs=(
            P(None, ("req", "head"), None),
            P("req", None, "head", None, None),
            P(),
            P(),
            P(),
            P(),
            P(None, "head", None),
            P("head"),
            P("head", None, None),
            P(),
            P(None, "head"),
            P("head", None),
        ),
        out_specs=(P(None, ("req", "head"), None), P(None, "req", None, "head", None)),
        check_vma=False,
    )
```

```python
import math

import jax
import jax.numpy as jnp
from jax import lax
from jax.sharding import PartitionSpec as P

EPSILON = 1e-05


def layer_norm(values, gain):
    average = jnp.mean(values, axis=-1, keepdims=True)
    centred = values - average
    variance = jnp.mean(centred * centred, axis=-1, keepdims=True)
    return centred * lax.rsqrt(variance + EPSILON) * gain.astype(jnp.float32)


def attend(queries, pairs, prefix_len, slopes, head_dim):
    stretch = queries.shape[0]
    prefix = pairs.shape[0] - stretch
    keys_part = pairs[..., :head_dim]
    values_part = pairs[..., head_dim:]
    scores = jnp.einsum("qhd,khd->hqk", queries, keys_part, preferred_element_type=jnp.float32) * (
        1.0 / math.sqrt(head_dim)
    )
    row_index = jnp.arange(stretch, dtype=jnp.int32)
    key_index = jnp.arange(prefix + stretch, dtype=jnp.int32)
    in_prefix = key_index < prefix
    query_pos = prefix_len + row_index
    key_pos = jnp.where(in_prefix, key_index, prefix_len + key_index - prefix)
    allowed = jnp.where(
        in_prefix[None, :],
        key_index[None, :] < prefix_len,
        (key_index - prefix)[None, :] <= row_index[:, None],
    )
    distance = (query_pos[:, None] - key_pos[None, :]).astype(jnp.float32)
    scores = scores - slopes[:, None, None] * distance[None]
    scores = jnp.where(allowed[None], scores, -jnp.inf)
    highest = jnp.max(scores, axis=-1, keepdims=True)
    expo = jnp.exp(scores - highest)
    soft = (expo / jnp.sum(expo, axis=-1, keepdims=True)).astype(jnp.bfloat16)
    context = jnp.einsum("hqk,khd->qhd", soft, values_part, preferred_element_type=jnp.float32)
    return context.astype(jnp.bfloat16).reshape(stretch, -1)


def head_sum(partial, head_count, stretch_rows):
    inner_size = 4 if head_count % 4 == 0 else head_count
    outer_size = head_count // inner_size
    me = lax.axis_index("head")
    outer_me, inner_me = me // inner_size, me % inner_size
    blocks = partial.astype(jnp.bfloat16).reshape(
        partial.shape[:2] + (outer_size, inner_size, stretch_rows) + partial.shape[3:]
    )
    level_one = lax.dynamic_index_in_dim(blocks, inner_me, 3, False).astype(jnp.float32)
    for shift in range(1, inner_size):
        pairs = [(j, (j // inner_size) * inner_size + (j % inner_size + shift) % inner_size) for j in range(head_count)]
        sent = lax.dynamic_index_in_dim(blocks, (inner_me + shift) % inner_size, 3, False)
        level_one = level_one + lax.ppermute(sent, "head", pairs).astype(jnp.float32)
    rounded_one = level_one.astype(jnp.bfloat16)
    total = lax.dynamic_index_in_dim(level_one, outer_me, 2, False)
    for shift in range(1, outer_size):
        pairs = [(j, ((j // inner_size + shift) % outer_size) * inner_size + j % inner_size) for j in range(head_count)]
        sent = lax.dynamic_index_in_dim(rounded_one, (outer_me + shift) % outer_size, 2, False)
        total = total + lax.ppermute(sent, "head", pairs).astype(jnp.float32)
    return total


def head_gather(rows, head_count):
    inner_size = 4 if head_count % 4 == 0 else head_count
    outer_size = head_count // inner_size
    me = lax.axis_index("head")
    outer_me, inner_me = me // inner_size, me % inner_size
    held = [rows]
    for shift in range(1, outer_size):
        pairs = [(j, ((j // inner_size + shift) % outer_size) * inner_size + j % inner_size) for j in range(head_count)]
        held.append(lax.ppermute(rows, "head", pairs))
    by_outer = jnp.take(jnp.stack(held), (outer_me - jnp.arange(outer_size)) % outer_size, axis=0)
    held = [by_outer]
    for shift in range(1, inner_size):
        pairs = [(j, (j // inner_size) * inner_size + (j % inner_size + shift) % inner_size) for j in range(head_count)]
        held.append(lax.ppermute(by_outer, "head", pairs))
    by_inner = jnp.take(jnp.stack(held), (inner_me - jnp.arange(inner_size)) % inner_size, axis=0)
    gathered = jnp.moveaxis(by_inner, (0, 1), (3, 2))
    return gathered.reshape(rows.shape[:2] + (head_count * rows.shape[2],) + rows.shape[3:])


def land(incoming, req_count, head_count):
    shape = (req_count, head_count) + incoming.shape[1:]
    landed = incoming.reshape(shape).transpose(0, 2, 1, 3, 4, 5)
    return landed.reshape(landed.shape[:2] + (-1,) + landed.shape[4:])


def local(
    stretch_acts,
    cache_prefill,
    stretch_lens,
    prefix_lens,
    req_order,
    attn_gain,
    in_weight,
    slopes,
    out_weight,
    mlp_gain,
    up_weight,
    down_weight,
):
    req_count = lax.axis_size("req")
    head_count = lax.axis_size("head")
    req_index = lax.axis_index("req")
    head_index = lax.axis_index("head")
    requests = stretch_acts.shape[0]
    stretch_rows = stretch_acts.shape[1]
    features = stretch_acts.shape[2]
    group_size = requests // req_count
    span_rows = head_count * stretch_rows
    stretch_max = req_count * span_rows
    prefix_rows = cache_prefill.shape[2]
    heads_here = in_weight.shape[1]
    pair_width = cache_prefill.shape[4]
    head_dim = pair_width // 2
    members = lax.dynamic_slice_in_dim(req_order, req_index * group_size, group_size)
    member_stretch = jnp.take(stretch_lens, members)
    member_prefix = jnp.take(prefix_lens, members)
    ordered_prefix = jnp.take(prefix_lens, req_order)
    positions = head_index * prefix_rows + jnp.arange(prefix_rows, dtype=jnp.int32)
    keep = positions[None, :] < ordered_prefix[:, None]
    local_layers = cache_prefill.shape[0]
    slots = cache_prefill.shape[1]
    heads = cache_prefill.shape[3]
    devices = req_count * head_count
    chunks = []
    deferred = []
    later_layers = cache_prefill[1:]
    for layer in range(local_layers):
        source = cache_prefill[0] if layer == 0 else later_layers[layer - 1]
        dealt_cache = jnp.where(
            keep[:, :, None, None],
            jnp.take(source, req_order, axis=0),
            jnp.zeros((), cache_prefill.dtype),
        )
        outgoing = (
            dealt_cache.reshape(req_count, group_size, prefix_rows, head_count, heads // head_count, pair_width)
            .transpose(0, 3, 1, 2, 4, 5)
            .reshape(devices, group_size, prefix_rows, heads // head_count, pair_width)
        )
        if layer == 0:
            incoming = lax.all_to_all(outgoing, ("req", "head"), 0, 0, tiled=True)
            incoming, later_layers = lax.optimization_barrier((incoming, later_layers))
            chunks.append(land(incoming, req_count, head_count))
        else:
            deferred.append(outgoing)
    current = chunks[0][0]
    dealt_acts = jnp.take(stretch_acts, req_order, axis=0)
    dealt_rows = lax.all_to_all(dealt_acts, "req", split_axis=0, concat_axis=1, tiled=True).reshape(
        group_size, req_count, stretch_rows, features
    )
    gathered = lax.all_gather(dealt_rows, "head", axis=2, tiled=True)
    normed = (
        layer_norm(gathered.astype(jnp.float32), attn_gain)
        .astype(jnp.bfloat16)
        .reshape(group_size * stretch_max, features)
    )
    mixed = jnp.dot(
        normed,
        in_weight.reshape(features, heads_here * 3 * head_dim),
        preferred_element_type=jnp.float32,
    )
    mixed = mixed.reshape(group_size, stretch_max, heads_here, 3 * head_dim).astype(jnp.bfloat16)
    attn_sums = []
    for member in range(group_size):
        pairs = jnp.concatenate([current[member], mixed[member, :, :, head_dim:]], axis=0)
        context = attend(mixed[member, :, :, :head_dim], pairs, member_prefix[member], slopes, head_dim)
        partial_attn = jnp.dot(
            context,
            out_weight.reshape(heads_here * head_dim, features),
            preferred_element_type=jnp.float32,
        )
        partial_attn = partial_attn.reshape(1, req_count, span_rows, features)
        attn_sums.append(head_sum(partial_attn, head_count, stretch_rows))
    attn_rows = jnp.concatenate(attn_sums, axis=0)
    residual_rows = dealt_rows.astype(jnp.float32) + attn_rows
    normed_rows = layer_norm(residual_rows, mlp_gain).astype(jnp.bfloat16)
    normed_all = head_gather(normed_rows, head_count)
    deferred, normed_all = lax.optimization_barrier((deferred, normed_all))
    for outgoing in deferred:
        chunks.append(land(lax.all_to_all(outgoing, ("req", "head"), 0, 0, tiled=True), req_count, head_count))
    relaid = jnp.stack(chunks, axis=1).reshape((req_count * local_layers,) + chunks[0].shape[1:])
    member_sums = []
    for member in range(group_size):
        inner = jax.nn.gelu(
            jnp.dot(
                normed_all[member].reshape(stretch_max, features),
                up_weight,
                preferred_element_type=jnp.float32,
            ),
            approximate=False,
        ).astype(jnp.bfloat16)
        partial_mlp = jnp.dot(inner, down_weight, preferred_element_type=jnp.float32).reshape(
            1, req_count, span_rows, features
        )
        member_sums.append(head_sum(partial_mlp, head_count, stretch_rows))
    mlp_rows = jnp.concatenate(member_sums, axis=0)
    relaid, mlp_rows = lax.optimization_barrier((relaid, mlp_rows))
    row_number = (
        jnp.arange(req_count, dtype=jnp.int32)[:, None] * head_count + head_index
    ) * stretch_rows + jnp.arange(stretch_rows, dtype=jnp.int32)[None, :]
    usable = row_number[None] < member_stretch[:, None, None]
    result = jnp.where(
        usable[..., None], residual_rows + mlp_rows, jnp.zeros((), jnp.float32)
    ).astype(jnp.bfloat16)
    returned = lax.all_to_all(result, "req", split_axis=1, concat_axis=0, tiled=True).reshape(
        requests, stretch_rows, features
    )
    inverse = jnp.argsort(req_order)
    layer_out = jnp.take(returned, inverse, axis=0)
    return (layer_out, relaid)


def solution(mesh):
    return jax.shard_map(
        local,
        mesh=mesh,
        in_specs=(
            P(None, ("req", "head"), None),
            P("req", None, "head", None, None),
            P(),
            P(),
            P(),
            P(),
            P(None, "head", None),
            P("head"),
            P("head", None, None),
            P(),
            P(None, "head"),
            P("head", None),
        ),
        out_specs=(P(None, ("req", "head"), None), P(None, "req", None, "head", None)),
        check_vma=False,
    )
```
